128 devices in a mesh: wave: 8 (over z, x_hi), angle: 16 (over x_lo, y, core).
Axes of the slice: x: 4 (x_hi: 2, x_lo: 2; x = x_hi * 2 + x_lo), y: 4, z: 4, core: 2. Of those that a mesh axis runs over, the one named last changes fastest.
Arguments:
- hologram_real: bfloat16 [32, 16, 512, 512], P('wave', 'angle'), may hold values from -6 to 6
- hologram_imaginary: bfloat16 [32, 16, 512, 512], P('wave', 'angle'), may hold values from -6 to 6
- pair_slot: int32 [2, 32], P(None, 'wave'), may hold values from 0 to 3
- kernel_real: bfloat16 [32, 2, 16, 128], replicated, may hold values from -0.1875 to 0.1875
- kernel_imaginary: bfloat16 [32, 2, 16, 128], replicated, may hold values from -0.1875 to 0.1875
Outputs:
- volume_real: float32 [512, 512, 128], P('angle', 'wave')
- volume_imaginary: float32 [512, 512, 128], P('angle', 'wave')
The draws below stay inside these ranges and needn't reach their ends.
Inputs may be any that keep to these rules, and one draw needn't show every extreme that they name: pair_slot[s, w] is a slot of the wavelength group whose index differs from w's group in bit s; every group has 4 wavelengths.
All inputs are finite; a program needn't handle non-finite values.
Results may differ from the reference program's by a relative error of at most 0.0067.
Values may be sent and summed in bfloat16 or wider, within the bound.
No kernel may reach another device: no remote copies, remote signals or barrier semaphores. Data moves between devices by JAX's collectives and lax.ppermute only.
A program may use at most 128 MiB of HBM per device.

```python
import math
import jax
import jax.numpy as jnp
from jax import lax

ROWS = 512
COLS = 512
DEPTH = 128
WAVE_DEV = 4
SECTIONS = 2
WAVES = 32
ANGLES = 16


def with_ends(entries, rng, low, largest):
    place = [jax.random.randint(jax.random.fold_in(rng, axis), (), 0, length) for axis, length in enumerate(entries.shape)]
    widest = entries.shape.index(max(entries.shape))
    beside = place[:widest] + [(place[widest] + 1) % entries.shape[widest]] + place[widest + 1:]
    return entries.at[tuple(place)].set(low).at[tuple(beside)].set(largest)


def shard_levels(key, extent, split, least, top_value):
    loudness, own = 1.0, jax.random.fold_in(key, 6)
    for axis_at, parts in split:
        steps = jnp.exp(jax.random.uniform(jax.random.fold_in(own, axis_at), (parts,), jnp.float32, least / len(split), top_value / len(split)))
        loudness = loudness * jnp.repeat(steps, extent[axis_at] // parts).reshape([-1 if axis == axis_at else 1 for axis in range(len(extent))])
    return loudness


def gaussian(stream_key, shape, spread, bound, pieces=(), kind=jnp.bfloat16):
    array = spread * jax.random.normal(stream_key, shape, jnp.float32)
    if pieces:
        array = array * shard_levels(stream_key, shape, pieces, -0.22, 0.18)
    return jnp.clip(array, -bound, bound).astype(kind)


def setup_inputs(seed: int = 0) -> dict:
    seeds = jax.random.split(jax.random.key(seed), 6)
    hologram_real = gaussian(seeds[0], (WAVES, ANGLES, ROWS, COLS), 1.0, 6.0, ((0, 8), (1, 16)))
    hologram_imaginary = gaussian(seeds[1], (WAVES, ANGLES, ROWS, COLS), 1.0, 6.0, ((0, 8), (1, 16)))
    pair_slot = with_ends(jax.random.randint(seeds[2], (SECTIONS, WAVES), 0, WAVE_DEV), jax.random.fold_in(seeds[2], 1), 0, WAVE_DEV - 1).astype(jnp.int32)
    kernel_real = gaussian(seeds[3], (WAVES, SECTIONS, ANGLES, DEPTH), (WAVES * SECTIONS * ANGLES) ** -0.5, 0.1875)
    kernel_imaginary = gaussian(seeds[4], (WAVES, SECTIONS, ANGLES, DEPTH), (WAVES * SECTIONS * ANGLES) ** -0.5, 0.1875)
    return {"hologram_real": hologram_real, "hologram_imaginary": hologram_imaginary, "pair_slot": pair_slot, "kernel_real": kernel_real, "kernel_imaginary": kernel_imaginary}


def dft_tables(length):
    counter = jnp.arange(length, dtype=jnp.int32)
    product = counter[:, None] * counter[None, :] % length
    phase = product.astype(jnp.float32) * (2.0 * math.pi / length)
    factor = 1.0 / math.sqrt(length)
    return ((jnp.cos(phase) * factor).astype(jnp.bfloat16), (-jnp.sin(phase) * factor).astype(jnp.bfloat16))

def spectrum(field_real, field_imag, row_tables, col_tables):
    first = field_real.astype(jnp.float32)
    second = field_imag.astype(jnp.float32)
    col_real = col_tables[0].astype(jnp.float32)
    col_imag = col_tables[1].astype(jnp.float32)
    half_real = (jnp.einsum('mrc,ck->mrk', first, col_real) - jnp.einsum('mrc,ck->mrk', second, col_imag)).astype(jnp.bfloat16)
    half_imag = (jnp.einsum('mrc,ck->mrk', first, col_imag) + jnp.einsum('mrc,ck->mrk', second, col_real)).astype(jnp.bfloat16)
    row_real = row_tables[0].astype(jnp.float32)
    row_imag = row_tables[1].astype(jnp.float32)
    third = half_real.astype(jnp.float32)
    fourth = half_imag.astype(jnp.float32)
    out_real = (jnp.einsum('rq,mqk->mrk', row_real, third) - jnp.einsum('rq,mqk->mrk', row_imag, fourth)).astype(jnp.bfloat16)
    out_imag = (jnp.einsum('rq,mqk->mrk', row_real, fourth) + jnp.einsum('rq,mqk->mrk', row_imag, third)).astype(jnp.bfloat16)
    return (out_real, out_imag)

def reference(hologram_real, hologram_imaginary, pair_slot, kernel_real, kernel_imaginary):
    row_tables = dft_tables(ROWS)
    col_tables = dft_tables(COLS)

    def one_wave(carry, wave_number):
        volume_real, volume_imag = carry
        own_real = lax.dynamic_index_in_dim(hologram_real, wave_number, 0, keepdims=False).astype(jnp.float32)
        own_imag = lax.dynamic_index_in_dim(hologram_imaginary, wave_number, 0, keepdims=False).astype(jnp.float32)
        group = wave_number // WAVE_DEV
        kern_real = lax.dynamic_index_in_dim(kernel_real, wave_number, 0, keepdims=False).astype(jnp.float32)
        kern_imag = lax.dynamic_index_in_dim(kernel_imaginary, wave_number, 0, keepdims=False).astype(jnp.float32)
        for section_number in range(SECTIONS):
            slot = lax.dynamic_index_in_dim(pair_slot[section_number], wave_number, 0, keepdims=False)
            partner = (jnp.bitwise_xor(group, 1 << section_number) * WAVE_DEV + slot).astype(jnp.int32)
            other_real = lax.dynamic_index_in_dim(hologram_real, partner, 0, keepdims=False).astype(jnp.float32)
            other_imag = lax.dynamic_index_in_dim(hologram_imaginary, partner, 0, keepdims=False).astype(jnp.float32)
            synth_real = (own_real * other_real + own_imag * other_imag).astype(jnp.bfloat16)
            synth_imag = (own_imag * other_real - own_real * other_imag).astype(jnp.bfloat16)
            spec_real, spec_imag = spectrum(synth_real, synth_imag, row_tables, col_tables)
            spec_real = spec_real.astype(jnp.float32)
            spec_imag = spec_imag.astype(jnp.float32)
            weight_real = kern_real[section_number]
            weight_imag = kern_imag[section_number]
            volume_real = volume_real + jnp.einsum('ark,az->rkz', spec_real, weight_real) - jnp.einsum('ark,az->rkz', spec_imag, weight_imag)
            volume_imag = volume_imag + jnp.einsum('ark,az->rkz', spec_real, weight_imag) + jnp.einsum('ark,az->rkz', spec_imag, weight_real)
        return ((volume_real, volume_imag), None)
    start = (jnp.zeros((ROWS, COLS, DEPTH), jnp.float32), jnp.zeros((ROWS, COLS, DEPTH), jnp.float32))
    result, _ = lax.scan(one_wave, start, jnp.arange(WAVES, dtype=jnp.int32))
    return (result[0], result[1])
```

```python
import math

import jax
import jax.numpy as jnp
from jax import lax
from jax.sharding import PartitionSpec as P


def from_partner(block, axis, bit):
    count = lax.axis_size(axis)
    route = []
    for low in range(count):
        high = low | 1 << bit
        if high != low and high < count:
            route += [(low, high), (high, low)]
    return lax.ppermute(block, axis, route)


def dft_tables(length):
    counter = jnp.arange(length, dtype=jnp.int32)
    product = counter[:, None] * counter[None, :] % length
    phase = product.astype(jnp.float32) * (2.0 * math.pi / length)
    factor = 1.0 / math.sqrt(length)
    return (
        (jnp.cos(phase) * factor).astype(jnp.bfloat16),
        (-jnp.sin(phase) * factor).astype(jnp.bfloat16),
    )


def complex_block(table_real, table_imag):
    top = jnp.stack([table_real, table_imag], axis=1)
    bottom = jnp.stack([-table_imag, table_real], axis=1)
    return jnp.stack([top, bottom], axis=0)


def shards(hologram_real, hologram_imaginary, pair_slot, kernel_real, kernel_imaginary):
    fp = jnp.float32
    wave_devices = lax.axis_size("wave")
    angle_devices = lax.axis_size("angle")
    local_waves, local_angles, row_count, col_count = hologram_real.shape
    section_count = pair_slot.shape[0]
    depth_count = kernel_real.shape[3]
    row_real, row_imag = dft_tables(row_count)
    col_real, col_imag = dft_tables(col_count)
    own_real = hologram_real[:, 0].astype(fp)
    own_imag = hologram_imaginary[:, 0].astype(fp)
    synth = []
    for section_number in range(section_count):
        got_real, got_imag = from_partner(
            (hologram_real, hologram_imaginary), "wave", section_number
        )
        other_real = jnp.take(got_real[:, 0], pair_slot[section_number], axis=0).astype(fp)
        other_imag = jnp.take(got_imag[:, 0], pair_slot[section_number], axis=0).astype(fp)
        synth_real = (own_real * other_real + own_imag * other_imag).astype(jnp.bfloat16)
        synth_imag = (own_imag * other_real - own_real * other_imag).astype(jnp.bfloat16)
        synth.append(jnp.stack([synth_real, synth_imag], axis=2))
    field = jnp.stack(synth, axis=1).reshape(-1, row_count, 2, col_count)
    col_block = complex_block(col_real, col_imag)
    half = jnp.einsum(
        "mqpc,pcdk->mqdk", field, col_block, preferred_element_type=fp
    ).astype(jnp.bfloat16)
    row_block = jnp.transpose(complex_block(row_real, row_imag), (2, 3, 0, 1))
    spec = jnp.einsum(
        "erdq,mqdk->rmek", row_block, half, preferred_element_type=fp
    ).astype(jnp.bfloat16)
    field_count = spec.shape[1]
    rows_per = row_count // angle_devices
    cols_per = col_count // wave_devices
    send = spec.reshape(angle_devices, rows_per, field_count, 2, wave_devices, cols_per)
    send = jnp.transpose(send, (4, 0, 1, 2, 3, 5)).reshape(
        wave_devices * angle_devices, rows_per, field_count, 2, cols_per
    )
    got = lax.all_to_all(send, ("wave", "angle"), 0, 0, tiled=True)

    def all_weights(kernel_part):
        block = kernel_part.reshape(
            wave_devices, local_waves, section_count, angle_devices, depth_count
        )
        return jnp.transpose(block, (0, 3, 1, 2, 4)).reshape(
            wave_devices * angle_devices, local_waves * section_count, depth_count
        )

    weight = complex_block(all_weights(kernel_real), all_weights(kernel_imaginary))
    volume = jnp.einsum("srmck,csdmz->rkdz", got, weight, preferred_element_type=fp)
    return (volume[:, :, 0, :], volume[:, :, 1, :])


def solution(mesh):
    return jax.shard_map(
        shards,
        mesh=mesh,
        in_specs=(
            P("wave", "angle", None, None),
            P("wave", "angle", None, None),
            P(None, "wave"),
            P(),
            P(),
        ),
        out_specs=(P("angle", "wave", None), P("angle", "wave", None)),
        check_vma=False,
    )
```

```python
import functools
import math

import jax
import jax.numpy as jnp
from jax import lax
from jax.experimental import pallas as pl
from jax.experimental.pallas import tpu as pltpu
from jax.sharding import PartitionSpec as P


def from_partner(block, axis, bit):
    count = lax.axis_size(axis)
    route = []
    for low in range(count):
        high = low | 1 << bit
        if high != low and high < count:
            route += [(low, high), (high, low)]
    return lax.ppermute(block, axis, route)


def dft_tables(length):
    counter = jnp.arange(length, dtype=jnp.int32)
    product = counter[:, None] * counter[None, :] % length
    phase = product.astype(jnp.float32) * (2.0 * math.pi / length)
    factor = 1.0 / math.sqrt(length)
    return (
        (jnp.cos(phase) * factor).astype(jnp.bfloat16),
        (-jnp.sin(phase) * factor).astype(jnp.bfloat16),
    )


def column_tables(table_real, table_imag, blocks):
    rows = table_real.shape[0]
    er = table_real.reshape(rows, blocks, 1, -1)
    ei = table_imag.reshape(rows, blocks, 1, -1)

    def join(top, bottom):
        upper = jnp.concatenate(top, axis=2).reshape(rows, -1)
        lower = jnp.concatenate(bottom, axis=2).reshape(rows, -1)
        return jnp.concatenate([upper, lower], axis=0)

    first = join([er, ei], [-ei, er])
    second = join([-ei, er], [-er, -ei])
    return first, second


def spectrum_kernel(
    slot_ref, own_re, own_im, far_re, far_im, col_a, col_b, row_re, row_im, *rest
):
    out_ref = rest[-1]
    fp = jnp.float32
    bf = jnp.bfloat16
    a_re = own_re[0, 0].astype(fp)
    a_im = own_im[0, 0].astype(fp)
    b_re = far_re[0, 0].astype(fp)
    b_im = far_im[0, 0].astype(fp)
    z_re = (a_re * b_re + a_im * b_im).astype(bf)
    z_im = (a_im * b_re - a_re * b_im).astype(bf)
    n = z_re.shape[1]
    y_a = (
        jnp.dot(z_re, col_a[:n, :], preferred_element_type=fp)
        + jnp.dot(z_im, col_a[n:, :], preferred_element_type=fp)
    ).astype(bf)
    y_b = (
        jnp.dot(z_re, col_b[:n, :], preferred_element_type=fp)
        + jnp.dot(z_im, col_b[n:, :], preferred_element_type=fp)
    ).astype(bf)
    spec = (
        jnp.dot(row_re[...], y_a, preferred_element_type=fp)
        + jnp.dot(row_im[...], y_b, preferred_element_type=fp)
    ).astype(bf)
    blocks, groups, _, rows_per, lanes = out_ref.shape
    for block in range(blocks):
        out_ref[block, :, 0, :, :] = spec[:, block * lanes : (block + 1) * lanes].reshape(
            groups, rows_per, lanes
        )


def spectra(slots, own_re, own_im, far_re, far_im, col_a, col_b, row_re, row_im, blocks, groups, after):
    waves, _, rows, cols = own_re.shape
    lanes = 2 * cols // blocks
    rows_per = rows // groups
    field = pl.BlockSpec((1, 1, rows, cols), lambda i, sl: (i, 0, 0, 0))
    partner = pl.BlockSpec((1, 1, rows, cols), lambda i, sl: (sl[i], 0, 0, 0))
    whole_col = pl.BlockSpec((2 * cols, 2 * cols), lambda i, sl: (0, 0))
    whole_row = pl.BlockSpec((rows, rows), lambda i, sl: (0, 0))
    flops = waves * (2 * 2 * rows * (2 * cols) * (2 * cols) + 2 * 2 * rows * rows * (2 * cols))
    return pl.pallas_call(
        spectrum_kernel,
        out_shape=jax.ShapeDtypeStruct((blocks, groups, waves, rows_per, lanes), jnp.bfloat16),
        grid_spec=pltpu.PrefetchScalarGridSpec(
            num_scalar_prefetch=1,
            grid=(waves,),
            in_specs=[field, field, partner, partner, whole_col, whole_col, whole_row, whole_row]
            + [pl.BlockSpec(memory_space=pl.ANY)] * len(after),
            out_specs=pl.BlockSpec(
                (blocks, groups, 1, rows_per, lanes), lambda i, sl: (0, 0, i, 0, 0)
            ),
        ),
        compiler_params=pltpu.CompilerParams(vmem_limit_bytes=60 * 1024 * 1024),
        cost_estimate=pl.CostEstimate(
            flops=flops, transcendentals=0, bytes_accessed=waves * rows * cols * 12 + 12 * cols * cols
        ),
    )(slots, own_re, own_im, far_re, far_im, col_a, col_b, row_re, row_im, *after)


def shards(hologram_real, hologram_imaginary, pair_slot, kernel_real, kernel_imaginary):
    fp = jnp.float32
    wave_devices = lax.axis_size("wave")
    angle_devices = lax.axis_size("angle")
    local_waves, local_angles, row_count, col_count = hologram_real.shape
    section_count = pair_slot.shape[0]
    depth_count = kernel_real.shape[3]
    row_real, row_imag = dft_tables(row_count)
    col_real, col_imag = dft_tables(col_count)
    col_a, col_b = column_tables(col_real, col_imag, wave_devices)

    def all_weights(kernel_part):
        block = kernel_part.reshape(
            wave_devices, local_waves, section_count, angle_devices, depth_count
        )
        return jnp.transpose(block, (2, 0, 3, 1, 4)).reshape(
            section_count, wave_devices * angle_devices, local_waves, depth_count
        )

    k_re = all_weights(kernel_real)
    k_im = all_weights(kernel_imaginary)
    volume = None
    received = [
        from_partner((hologram_real, hologram_imaginary), "wave", section_number)
        for section_number in range(section_count)
    ]
    for section_number in range(section_count):
        got_real, got_imag = received[section_number]
        after = [a for other, got in enumerate(received) if other != section_number for a in got]
        send = spectra(
            pair_slot[section_number],
            hologram_real,
            hologram_imaginary,
            got_real,
            got_imag,
            col_a,
            col_b,
            row_real,
            row_imag,
            wave_devices,
            angle_devices,
            after,
        )
        send = send.reshape(wave_devices * angle_devices, *send.shape[2:])
        got = lax.all_to_all(send, ("wave", "angle"), 0, 0, tiled=True)
        kr = k_re[section_number]
        ki = k_im[section_number]
        w_first = jnp.stack([kr, ki], axis=2).reshape(kr.shape[0], kr.shape[1], -1)
        w_second = jnp.stack([-ki, kr], axis=2).reshape(kr.shape[0], kr.shape[1], -1)
        t_first = jnp.einsum("swrn,swx->rnx", got, w_first, preferred_element_type=fp)
        t_second = jnp.einsum("swrn,swx->rnx", got, w_second, preferred_element_type=fp)
        half = got.shape[3] // 2
        part = t_first[:, :half] + t_second[:, half:]
        volume = part if volume is None else volume + part
    volume = volume.reshape(volume.shape[0], volume.shape[1], 2, depth_count)
    return (volume[:, :, 0, :], volume[:, :, 1, :])


def solution(mesh):
    return jax.shard_map(
        shards,
        mesh=mesh,
        in_specs=(
            P("wave", "angle", None, None),
            P("wave", "angle", None, None),
            P(None, "wave"),
            P(),
            P(),
        ),
        out_specs=(P("angle", "wave", None), P("angle", "wave", None)),
        check_vma=False,
    )
```

```python
import functools
import math

import jax
import jax.numpy as jnp
from jax import lax
from jax.experimental import pallas as pl
from jax.experimental.pallas import tpu as pltpu
from jax.sharding import PartitionSpec as P


def from_partner(block, axis, bit):
    count = lax.axis_size(axis)
    route = []
    for low in range(count):
        high = low | 1 << bit
        if high != low and high < count:
            route += [(low, high), (high, low)]
    return lax.ppermute(block, axis, route)


def dft_tables(length):
    counter = jnp.arange(length, dtype=jnp.int32)
    product = counter[:, None] * counter[None, :] % length
    phase = product.astype(jnp.float32) * (2.0 * math.pi / length)
    factor = 1.0 / math.sqrt(length)
    return (
        (jnp.cos(phase) * factor).astype(jnp.bfloat16),
        (-jnp.sin(phase) * factor).astype(jnp.bfloat16),
    )


def column_tables(table_real, table_imag, blocks):
    rows = table_real.shape[0]
    er = table_real.reshape(rows, blocks, 1, -1)
    ei = table_imag.reshape(rows, blocks, 1, -1)

    def join(top, bottom):
        upper = jnp.concatenate(top, axis=2).reshape(rows, -1)
        lower = jnp.concatenate(bottom, axis=2).reshape(rows, -1)
        return jnp.concatenate([upper, lower], axis=0)

    first = join([er, ei], [-ei, er])
    second = join([-ei, er], [-er, -ei])
    return first, second


def spectrum_kernel(
    slot_ref, own_re, own_im, far_re, far_im, col_a, col_b, row_re, row_im, *rest
):
    out_ref = rest[-1]
    fp = jnp.float32
    bf = jnp.bfloat16
    a_re = own_re[0, 0].astype(fp)
    a_im = own_im[0, 0].astype(fp)
    b_re = far_re[0, 0].astype(fp)
    b_im = far_im[0, 0].astype(fp)
    z_re = (a_re * b_re + a_im * b_im).astype(bf)
    z_im = (a_im * b_re - a_re * b_im).astype(bf)
    n = z_re.shape[1]
    y_a = (
        jnp.dot(z_re, col_a[:n, :], preferred_element_type=fp)
        + jnp.dot(z_im, col_a[n:, :], preferred_element_type=fp)
    ).astype(bf)
    y_b = (
        jnp.dot(z_re, col_b[:n, :], preferred_element_type=fp)
        + jnp.dot(z_im, col_b[n:, :], preferred_element_type=fp)
    ).astype(bf)
    spec = (
        jnp.dot(row_re[...], y_a, preferred_element_type=fp)
        + jnp.dot(row_im[...], y_b, preferred_element_type=fp)
    ).astype(bf)
    blocks, groups, _, rows_per, lanes = out_ref.shape
    for block in range(blocks):
        out_ref[block, :, 0, :, :] = spec[:, block * lanes : (block + 1) * lanes].reshape(
            groups, rows_per, lanes
        )


def spectra(slots, own_re, own_im, far_re, far_im, col_a, col_b, row_re, row_im, blocks, groups, after):
    waves, _, rows, cols = own_re.shape
    lanes = 2 * cols // blocks
    rows_per = rows // groups
    field = pl.BlockSpec((1, 1, rows, cols), lambda i, sl: (i, 0, 0, 0))
    partner = pl.BlockSpec((1, 1, rows, cols), lambda i, sl: (sl[i], 0, 0, 0))
    whole_col = pl.BlockSpec((2 * cols, 2 * cols), lambda i, sl: (0, 0))
    whole_row = pl.BlockSpec((rows, rows), lambda i, sl: (0, 0))
    flops = waves * (2 * 2 * rows * (2 * cols) * (2 * cols) + 2 * 2 * rows * rows * (2 * cols))
    return pl.pallas_call(
        spectrum_kernel,
        out_shape=jax.ShapeDtypeStruct((blocks, groups, waves, rows_per, lanes), jnp.bfloat16),
        grid_spec=pltpu.PrefetchScalarGridSpec(
            num_scalar_prefetch=1,
            grid=(waves,),
            in_specs=[field, field, partner, partner, whole_col, whole_col, whole_row, whole_row]
            + [pl.BlockSpec(memory_space=pl.ANY)] * len(after),
            out_specs=pl.BlockSpec(
                (blocks, groups, 1, rows_per, lanes), lambda i, sl: (0, 0, i, 0, 0)
            ),
        ),
        compiler_params=pltpu.CompilerParams(vmem_limit_bytes=60 * 1024 * 1024),
        cost_estimate=pl.CostEstimate(
            flops=flops, transcendentals=0, bytes_accessed=waves * rows * cols * 12 + 12 * cols * cols
        ),
    )(slots, own_re, own_im, far_re, far_im, col_a, col_b, row_re, row_im, *after)


def shards(hologram_real, hologram_imaginary, pair_slot, kernel_real, kernel_imaginary):
    fp = jnp.float32
    wave_devices = lax.axis_size("wave")
    angle_devices = lax.axis_size("angle")
    local_waves, local_angles, row_count, col_count = hologram_real.shape
    section_count = pair_slot.shape[0]
    depth_count = kernel_real.shape[3]
    row_real, row_imag = dft_tables(row_count)
    col_real, col_imag = dft_tables(col_count)
    col_a, col_b = column_tables(col_real, col_imag, wave_devices)

    def all_weights(kernel_part):
        block = kernel_part.reshape(
            wave_devices, local_waves, section_count, angle_devices, depth_count
        )
        return jnp.transpose(block, (2, 0, 3, 1, 4)).reshape(
            section_count, wave_devices * angle_devices, local_waves, depth_count
        )

    k_re = all_weights(kernel_real)
    k_im = all_weights(kernel_imaginary)
    volume = None
    received = [
        from_partner((hologram_real, hologram_imaginary), "wave", section_number)
        for section_number in range(section_count)
    ]
    for section_number in range(section_count):
        got_real, got_imag = received[section_number]
        after = [a for other, got in enumerate(received) if other != section_number for a in got]
        send = spectra(
            pair_slot[section_number],
            hologram_real,
            hologram_imaginary,
            got_real,
            got_imag,
            col_a,
            col_b,
            row_real,
            row_imag,
            wave_devices,
            angle_devices,
            after,
        )
        send = send.reshape(wave_devices * angle_devices, *send.shape[2:])
        got = lax.all_to_all(send, ("wave", "angle"), 0, 0, tiled=True)
        got = got.reshape(-1, *got.shape[2:])
        kr = k_re[section_number].reshape(-1, depth_count)
        ki = k_im[section_number].reshape(-1, depth_count)
        weight = jnp.concatenate([kr, ki, -ki, kr], axis=1).T
        part = jnp.einsum("yk,krn->yrn", weight, got, preferred_element_type=fp)
        volume = part if volume is None else volume + part
    half = volume.shape[2] // 2
    out_count = volume.shape[0] // 2
    volume = volume[:out_count, :, :half] + volume[out_count:, :, half:]
    volume = jnp.transpose(volume.reshape(2, depth_count, *volume.shape[1:]), (2, 3, 0, 1))
    return (volume[:, :, 0, :], volume[:, :, 1, :])


def solution(mesh):
    return jax.shard_map(
        shards,
        mesh=mesh,
        in_specs=(
            P("wave", "angle", None, None),
            P("wave", "angle", None, None),
            P(None, "wave"),
            P(),
            P(),
        ),
        out_specs=(P("angle", "wave", None), P("angle", "wave", None)),
        check_vma=False,
    )
```

```python
import functools
import math

import jax
import jax.numpy as jnp
from jax import lax
from jax.experimental import pallas as pl
from jax.experimental.pallas import tpu as pltpu
from jax.sharding import PartitionSpec as P


def from_partner(block, axis, bit):
    count = lax.axis_size(axis)
    route = []
    for low in range(count):
        high = low | 1 << bit
        if high != low and high < count:
            route += [(low, high), (high, low)]
    return lax.ppermute(block, axis, route)


def dft_tables(length):
    counter = jnp.arange(length, dtype=jnp.int32)
    product = counter[:, None] * counter[None, :] % length
    phase = product.astype(jnp.float32) * (2.0 * math.pi / length)
    factor = 1.0 / math.sqrt(length)
    return (
        (jnp.cos(phase) * factor).astype(jnp.bfloat16),
        (-jnp.sin(phase) * factor).astype(jnp.bfloat16),
    )


def column_tables(table_real, table_imag, blocks):
    rows = table_real.shape[0]
    er = table_real.reshape(rows, blocks, 1, -1)
    ei = table_imag.reshape(rows, blocks, 1, -1)

    def join(top, bottom):
        upper = jnp.concatenate(top, axis=2).reshape(rows, -1)
        lower = jnp.concatenate(bottom, axis=2).reshape(rows, -1)
        return jnp.concatenate([upper, lower], axis=0)

    first = join([er, ei], [-ei, er])
    second = join([-ei, er], [-er, -ei])
    return first, second


def spectrum_kernel(
    slot_ref, own_re, own_im, far_re, far_im, col_a, col_b, row_re, row_im, *rest
):
    out_ref = rest[-1]
    fp = jnp.float32
    bf = jnp.bfloat16
    a_re = own_re[0, 0].astype(fp)
    a_im = own_im[0, 0].astype(fp)
    b_re = far_re[0, 0].astype(fp)
    b_im = far_im[0, 0].astype(fp)
    z_re = (a_re * b_re + a_im * b_im).astype(bf)
    z_im = (a_im * b_re - a_re * b_im).astype(bf)
    n = z_re.shape[1]
    y_a = (
        jnp.dot(z_re, col_a[:n, :], preferred_element_type=fp)
        + jnp.dot(z_im, col_a[n:, :], preferred_element_type=fp)
    ).astype(bf)
    y_b = (
        jnp.dot(z_re, col_b[:n, :], preferred_element_type=fp)
        + jnp.dot(z_im, col_b[n:, :], preferred_element_type=fp)
    ).astype(bf)
    spec = (
        jnp.dot(row_re[...], y_a, preferred_element_type=fp)
        + jnp.dot(row_im[...], y_b, preferred_element_type=fp)
    ).astype(bf)
    blocks, groups, _, rows_per, lanes = out_ref.shape
    for block in range(blocks):
        out_ref[block, :, 0, :, :] = spec[:, block * lanes : (block + 1) * lanes].reshape(
            groups, rows_per, lanes
        )


def spectra(
    slots, own_re, own_im, far_re, far_im, col_a, col_b, row_re, row_im, blocks, groups, after, first, waves
):
    _, _, rows, cols = own_re.shape
    lanes = 2 * cols // blocks
    rows_per = rows // groups
    field = pl.BlockSpec((1, 1, rows, cols), lambda i, sl: (first + i, 0, 0, 0))
    partner = pl.BlockSpec((1, 1, rows, cols), lambda i, sl: (sl[first + i], 0, 0, 0))
    whole_col = pl.BlockSpec((2 * cols, 2 * cols), lambda i, sl: (0, 0))
    whole_row = pl.BlockSpec((rows, rows), lambda i, sl: (0, 0))
    flops = waves * (2 * 2 * rows * (2 * cols) * (2 * cols) + 2 * 2 * rows * rows * (2 * cols))
    return pl.pallas_call(
        spectrum_kernel,
        out_shape=jax.ShapeDtypeStruct((blocks, groups, waves, rows_per, lanes), jnp.bfloat16),
        grid_spec=pltpu.PrefetchScalarGridSpec(
            num_scalar_prefetch=1,
            grid=(waves,),
            in_specs=[field, field, partner, partner, whole_col, whole_col, whole_row, whole_row]
            + [pl.BlockSpec(memory_space=pl.ANY)] * len(after),
            out_specs=pl.BlockSpec(
                (blocks, groups, 1, rows_per, lanes), lambda i, sl: (0, 0, i, 0, 0)
            ),
        ),
        compiler_params=pltpu.CompilerParams(vmem_limit_bytes=60 * 1024 * 1024),
        cost_estimate=pl.CostEstimate(
            flops=flops, transcendentals=0, bytes_accessed=waves * rows * cols * 12 + 12 * cols * cols
        ),
    )(slots, own_re, own_im, far_re, far_im, col_a, col_b, row_re, row_im, *after)


def shards(hologram_real, hologram_imaginary, pair_slot, kernel_real, kernel_imaginary):
    fp = jnp.float32
    wave_devices = lax.axis_size("wave")
    angle_devices = lax.axis_size("angle")
    local_waves, local_angles, row_count, col_count = hologram_real.shape
    section_count = pair_slot.shape[0]
    depth_count = kernel_real.shape[3]
    row_real, row_imag = dft_tables(row_count)
    col_real, col_imag = dft_tables(col_count)
    col_a, col_b = column_tables(col_real, col_imag, wave_devices)

    def all_weights(kernel_part):
        block = kernel_part.reshape(
            wave_devices, local_waves, section_count, angle_devices, depth_count
        )
        return jnp.transpose(block, (2, 0, 3, 1, 4)).reshape(
            section_count, wave_devices * angle_devices, local_waves, depth_count
        )

    k_re = all_weights(kernel_real)
    k_im = all_weights(kernel_imaginary)
    volume = None
    received = [
        from_partner((hologram_real, hologram_imaginary), "wave", section_number)
        for section_number in range(section_count)
    ]
    pieces = 2
    per_piece = local_waves // pieces
    for section_number in range(section_count):
        got_real, got_imag = received[section_number]
        after = [a for other, got in enumerate(received) if other != section_number for a in got]
        for piece in range(pieces):
            first = piece * per_piece
            send = spectra(
                pair_slot[section_number],
                hologram_real,
                hologram_imaginary,
                got_real,
                got_imag,
                col_a,
                col_b,
                row_real,
                row_imag,
                wave_devices,
                angle_devices,
                after,
                first,
                per_piece,
            )
            send = send.reshape(wave_devices * angle_devices, *send.shape[2:])
            got = lax.all_to_all(send, ("wave", "angle"), 0, 0, tiled=True)
            got = got.reshape(-1, got.shape[2], 2, got.shape[3] // 2)
            kr = k_re[section_number][:, first : first + per_piece].reshape(-1, depth_count)
            ki = k_im[section_number][:, first : first + per_piece].reshape(-1, depth_count)
            weight = jnp.stack(
                [jnp.concatenate([kr, ki], axis=1), jnp.concatenate([-ki, kr], axis=1)], axis=1
            )
            part = jnp.einsum("kreq,kex->rqx", got, weight, preferred_element_type=fp)
            volume = part if volume is None else volume + part
    return (volume[:, :, :depth_count], volume[:, :, depth_count:])


def solution(mesh):
    return jax.shard_map(
        shards,
        mesh=mesh,
        in_specs=(
            P("wave", "angle", None, None),
            P("wave", "angle", None, None),
            P(None, "wave"),
            P(),
            P(),
        ),
        out_specs=(P("angle", "wave", None), P("angle", "wave", None)),
        check_vma=False,
    )
```

```python
import functools
import math

import jax
import jax.numpy as jnp
from jax import lax
from jax.experimental import pallas as pl
from jax.experimental.pallas import tpu as pltpu
from jax.sharding import PartitionSpec as P


def from_partner(block, axis, bit):
    count = lax.axis_size(axis)
    route = []
    for low in range(count):
        high = low | 1 << bit
        if high != low and high < count:
            route += [(low, high), (high, low)]
    return lax.ppermute(block, axis, route)


def dft_tables(length):
    counter = jnp.arange(length, dtype=jnp.int32)
    product = counter[:, None] * counter[None, :] % length
    phase = product.astype(jnp.float32) * (2.0 * math.pi / length)
    factor = 1.0 / math.sqrt(length)
    return (
        (jnp.cos(phase) * factor).astype(jnp.bfloat16),
        (-jnp.sin(phase) * factor).astype(jnp.bfloat16),
    )


def column_tables(table_real, table_imag, blocks):
    rows = table_real.shape[0]
    er = table_real.reshape(rows, blocks, 1, -1)
    ei = table_imag.reshape(rows, blocks, 1, -1)

    def join(top, bottom):
        upper = jnp.concatenate(top, axis=2).reshape(rows, -1)
        lower = jnp.concatenate(bottom, axis=2).reshape(rows, -1)
        return jnp.concatenate([upper, lower], axis=0)

    return join([er, ei], [-ei, er])


def spectrum_kernel(
    slot_ref, own_re, own_im, far_re, far_im, col_a, row_re, row_im, *rest
):
    out_ref = rest[-1]
    fp = jnp.float32
    bf = jnp.bfloat16
    a_re = own_re[0, 0].astype(fp)
    a_im = own_im[0, 0].astype(fp)
    b_re = far_re[0, 0].astype(fp)
    b_im = far_im[0, 0].astype(fp)
    z_re = (a_re * b_re + a_im * b_im).astype(bf)
    z_im = (a_im * b_re - a_re * b_im).astype(bf)
    n = z_re.shape[1]
    y = (
        jnp.dot(z_re, col_a[:n, :], preferred_element_type=fp)
        + jnp.dot(z_im, col_a[n:, :], preferred_element_type=fp)
    ).astype(bf)
    first = jnp.dot(row_re[...], y, preferred_element_type=fp)
    second = jnp.dot(row_im[...], y, preferred_element_type=fp)
    blocks, groups, _, rows_per, lanes = out_ref.shape
    lane = lax.broadcasted_iota(jnp.int32, (first.shape[0], lanes), 1)
    for block in range(blocks):
        cut = slice(block * lanes, (block + 1) * lanes)
        swapped = pltpu.roll(second[:, cut], lanes // 2, 1)
        swapped = jnp.where(lane < lanes // 2, -swapped, swapped)
        spec = (first[:, cut] + swapped).astype(bf)
        out_ref[block, :, 0, :, :] = spec.reshape(groups, rows_per, lanes)


def spectra(slots, own_re, own_im, far_re, far_im, col_a, row_re, row_im, blocks, groups, after):
    waves, _, rows, cols = own_re.shape
    lanes = 2 * cols // blocks
    rows_per = rows // groups
    field = pl.BlockSpec((1, 1, rows, cols), lambda i, sl: (i, 0, 0, 0))
    partner = pl.BlockSpec((1, 1, rows, cols), lambda i, sl: (sl[i], 0, 0, 0))
    whole_col = pl.BlockSpec((2 * cols, 2 * cols), lambda i, sl: (0, 0))
    whole_row = pl.BlockSpec((rows, rows), lambda i, sl: (0, 0))
    flops = waves * (2 * rows * (2 * cols) * (2 * cols) + 2 * 2 * rows * rows * (2 * cols))
    return pl.pallas_call(
        spectrum_kernel,
        out_shape=jax.ShapeDtypeStruct((blocks, groups, waves, rows_per, lanes), jnp.bfloat16),
        grid_spec=pltpu.PrefetchScalarGridSpec(
            num_scalar_prefetch=1,
            grid=(waves,),
            in_specs=[field, field, partner, partner, whole_col, whole_row, whole_row]
            + [pl.BlockSpec(memory_space=pl.ANY)] * len(after),
            out_specs=pl.BlockSpec(
                (blocks, groups, 1, rows_per, lanes), lambda i, sl: (0, 0, i, 0, 0)
            ),
        ),
        compiler_params=pltpu.CompilerParams(vmem_limit_bytes=60 * 1024 * 1024),
        cost_estimate=pl.CostEstimate(
            flops=flops, transcendentals=0, bytes_accessed=waves * rows * cols * 12 + 12 * cols * cols
        ),
    )(slots, own_re, own_im, far_re, far_im, col_a, row_re, row_im, *after)


def shards(hologram_real, hologram_imaginary, pair_slot, kernel_real, kernel_imaginary):
    fp = jnp.float32
    wave_devices = lax.axis_size("wave")
    angle_devices = lax.axis_size("angle")
    local_waves, local_angles, row_count, col_count = hologram_real.shape
    section_count = pair_slot.shape[0]
    depth_count = kernel_real.shape[3]
    row_real, row_imag = dft_tables(row_count)
    col_real, col_imag = dft_tables(col_count)
    col_a = column_tables(col_real, col_imag, wave_devices)

    def all_weights(kernel_part):
        block = kernel_part.reshape(
            wave_devices, local_waves, section_count, angle_devices, depth_count
        )
        return jnp.transpose(block, (2, 0, 3, 1, 4)).reshape(
            section_count, wave_devices * angle_devices, local_waves, depth_count
        )

    k_re = all_weights(kernel_real)
    k_im = all_weights(kernel_imaginary)
    volume = None
    received = [
        from_partner((hologram_real, hologram_imaginary), "wave", section_number)
        for section_number in range(section_count)
    ]
    for section_number in range(section_count):
        got_real, got_imag = received[section_number]
        after = [a for other, got in enumerate(received) if other != section_number for a in got]
        send = spectra(
            pair_slot[section_number],
            hologram_real,
            hologram_imaginary,
            got_real,
            got_imag,
            col_a,
            row_real,
            row_imag,
            wave_devices,
            angle_devices,
            after,
        )
        send = send.reshape(wave_devices * angle_devices, *send.shape[2:])
        got = lax.all_to_all(send, ("wave", "angle"), 0, 0, tiled=True)
        kr = k_re[section_number]
        ki = k_im[section_number]
        w_first = jnp.stack([kr, ki], axis=2).reshape(kr.shape[0], kr.shape[1], -1)
        w_second = jnp.stack([-ki, kr], axis=2).reshape(kr.shape[0], kr.shape[1], -1)
        t_first = jnp.einsum("swrn,swx->rnx", got, w_first, preferred_element_type=fp)
        t_second = jnp.einsum("swrn,swx->rnx", got, w_second, preferred_element_type=fp)
        half = got.shape[3] // 2
        part = t_first[:, :half] + t_second[:, half:]
        volume = part if volume is None else volume + part
    volume = volume.reshape(volume.shape[0], volume.shape[1], 2, depth_count)
    return (volume[:, :, 0, :], volume[:, :, 1, :])


def solution(mesh):
    return jax.shard_map(
        shards,
        mesh=mesh,
        in_specs=(
            P("wave", "angle", None, None),
            P("wave", "angle", None, None),
            P(None, "wave"),
            P(),
            P(),
        ),
        out_specs=(P("angle", "wave", None), P("angle", "wave", None)),
        check_vma=False,
    )
```

```python
import functools
import math

import jax
import jax.numpy as jnp
from jax import lax
from jax.experimental import pallas as pl
from jax.experimental.pallas import tpu as pltpu
from jax.sharding import PartitionSpec as P


def from_partner(block, axis, bit):
    count = lax.axis_size(axis)
    route = []
    for low in range(count):
        high = low | 1 << bit
        if high != low and high < count:
            route += [(low, high), (high, low)]
    return lax.ppermute(block, axis, route)


def dft_tables(length):
    counter = jnp.arange(length, dtype=jnp.int32)
    product = counter[:, None] * counter[None, :] % length
    phase = product.astype(jnp.float32) * (2.0 * math.pi / length)
    factor = 1.0 / math.sqrt(length)
    return (
        (jnp.cos(phase) * factor).astype(jnp.bfloat16),
        (-jnp.sin(phase) * factor).astype(jnp.bfloat16),
    )


def column_tables(table_real, table_imag, blocks):
    rows = table_real.shape[0]
    er = table_real.reshape(rows, blocks, 1, -1)
    ei = table_imag.reshape(rows, blocks, 1, -1)

    def join(top, bottom):
        upper = jnp.concatenate(top, axis=2).reshape(rows, -1)
        lower = jnp.concatenate(bottom, axis=2).reshape(rows, -1)
        return jnp.concatenate([upper, lower], axis=0)

    return join([er, ei], [-ei, er])


def spectrum_kernel(
    slot_ref, own_re, own_im, far_re, far_im, col_a, row_re, row_im, *rest
):
    out_ref = rest[-1]
    fp = jnp.float32
    bf = jnp.bfloat16
    a_re = own_re[0, 0].astype(fp)
    a_im = own_im[0, 0].astype(fp)
    b_re = far_re[0, 0].astype(fp)
    b_im = far_im[0, 0].astype(fp)
    z_re = (a_re * b_re + a_im * b_im).astype(bf)
    z_im = (a_im * b_re - a_re * b_im).astype(bf)
    n = z_re.shape[1]
    y = (
        jnp.dot(z_re, col_a[:n, :], preferred_element_type=fp)
        + jnp.dot(z_im, col_a[n:, :], preferred_element_type=fp)
    ).astype(bf)
    first = jnp.dot(row_re[...], y, preferred_element_type=fp)
    second = jnp.dot(row_im[...], y, preferred_element_type=fp)
    blocks, groups, _, rows_per, lanes = out_ref.shape
    lane = lax.broadcasted_iota(jnp.int32, (first.shape[0], lanes), 1)
    for block in range(blocks):
        cut = slice(block * lanes, (block + 1) * lanes)
        swapped = pltpu.roll(second[:, cut], lanes // 2, 1)
        swapped = jnp.where(lane < lanes // 2, -swapped, swapped)
        spec = (first[:, cut] + swapped).astype(bf)
        out_ref[block, :, 0, :, :] = spec.reshape(groups, rows_per, lanes)


def spectra(slots, own_re, own_im, far_re, far_im, col_a, row_re, row_im, blocks, groups, after):
    waves, _, rows, cols = own_re.shape
    lanes = 2 * cols // blocks
    rows_per = rows // groups
    field = pl.BlockSpec((1, 1, rows, cols), lambda i, sl: (i, 0, 0, 0))
    partner = pl.BlockSpec((1, 1, rows, cols), lambda i, sl: (sl[i], 0, 0, 0))
    whole_col = pl.BlockSpec((2 * cols, 2 * cols), lambda i, sl: (0, 0))
    whole_row = pl.BlockSpec((rows, rows), lambda i, sl: (0, 0))
    flops = waves * (2 * rows * (2 * cols) * (2 * cols) + 2 * 2 * rows * rows * (2 * cols))
    return pl.pallas_call(
        spectrum_kernel,
        out_shape=jax.ShapeDtypeStruct((blocks, groups, waves, rows_per, lanes), jnp.bfloat16),
        grid_spec=pltpu.PrefetchScalarGridSpec(
            num_scalar_prefetch=1,
            grid=(waves,),
            in_specs=[field, field, partner, partner, whole_col, whole_row, whole_row]
            + [pl.BlockSpec(memory_space=pl.ANY)] * len(after),
            out_specs=pl.BlockSpec(
                (blocks, groups, 1, rows_per, lanes), lambda i, sl: (0, 0, i, 0, 0)
            ),
        ),
        compiler_params=pltpu.CompilerParams(vmem_limit_bytes=60 * 1024 * 1024),
        cost_estimate=pl.CostEstimate(
            flops=flops, transcendentals=0, bytes_accessed=waves * rows * cols * 12 + 12 * cols * cols
        ),
    )(slots, own_re, own_im, far_re, far_im, col_a, row_re, row_im, *after)


def shards(hologram_real, hologram_imaginary, pair_slot, kernel_real, kernel_imaginary):
    fp = jnp.float32
    wave_devices = lax.axis_size("wave")
    angle_devices = lax.axis_size("angle")
    local_waves, local_angles, row_count, col_count = hologram_real.shape
    section_count = pair_slot.shape[0]
    depth_count = kernel_real.shape[3]
    row_real, row_imag = dft_tables(row_count)
    col_real, col_imag = dft_tables(col_count)
    col_a = column_tables(col_real, col_imag, wave_devices)

    def all_weights(kernel_part):
        block = kernel_part.reshape(
            wave_devices, local_waves, section_count, angle_devices, depth_count
        )
        return jnp.transpose(block, (2, 0, 3, 1, 4)).reshape(
            section_count, wave_devices * angle_devices, local_waves, depth_count
        )

    k_re = all_weights(kernel_real)
    k_im = all_weights(kernel_imaginary)
    volume = None
    received = [
        from_partner((hologram_real, hologram_imaginary), "wave", section_number)
        for section_number in range(section_count)
    ]
    for section_number in range(section_count):
        got_real, got_imag = received[section_number]
        after = [a for other, got in enumerate(received) if other != section_number for a in got]
        send = spectra(
            pair_slot[section_number],
            hologram_real,
            hologram_imaginary,
            got_real,
            got_imag,
            col_a,
            row_real,
            row_imag,
            wave_devices,
            angle_devices,
            after,
        )
        send = send.reshape(wave_devices * angle_devices, *send.shape[2:])
        got = lax.all_to_all(send, ("wave", "angle"), 0, 0, tiled=True)
        kr = k_re[section_number]
        ki = k_im[section_number]
        w_first = jnp.stack([kr, ki], axis=2).reshape(kr.shape[0], kr.shape[1], -1)
        w_second = jnp.stack([-ki, kr], axis=2).reshape(kr.shape[0], kr.shape[1], -1)
        t_first = jnp.einsum("swrn,swx->rnx", got, w_first, preferred_element_type=fp)
        t_second = jnp.einsum("swrn,swx->rnx", got, w_second, preferred_element_type=fp)
        half = got.shape[3] // 2
        part = t_first[:, :half] + t_second[:, half:]
        volume = part if volume is None else volume + part
    return (volume[:, :, :depth_count], volume[:, :, depth_count:])


def solution(mesh):
    return jax.shard_map(
        shards,
        mesh=mesh,
        in_specs=(
            P("wave", "angle", None, None),
            P("wave", "angle", None, None),
            P(None, "wave"),
            P(),
            P(),
        ),
        out_specs=(P("angle", "wave", None), P("angle", "wave", None)),
        check_vma=False,
    )
```

```python
import functools
import math

import jax
import jax.numpy as jnp
from jax import lax
from jax.experimental import pallas as pl
from jax.experimental.layout import Layout, with_layout_constraint
from jax.experimental.pallas import tpu as pltpu
from jax.sharding import PartitionSpec as P


def from_partner(block, axis, bit):
    count = lax.axis_size(axis)
    route = []
    for low in range(count):
        high = low | 1 << bit
        if high != low and high < count:
            route += [(low, high), (high, low)]
    return lax.ppermute(block, axis, route)


def dft_tables(length):
    counter = jnp.arange(length, dtype=jnp.int32)
    product = counter[:, None] * counter[None, :] % length
    phase = product.astype(jnp.float32) * (2.0 * math.pi / length)
    factor = 1.0 / math.sqrt(length)
    return (
        (jnp.cos(phase) * factor).astype(jnp.bfloat16),
        (-jnp.sin(phase) * factor).astype(jnp.bfloat16),
    )


def column_tables(table_real, table_imag, blocks):
    rows = table_real.shape[0]
    er = table_real.reshape(rows, blocks, 1, -1)
    ei = table_imag.reshape(rows, blocks, 1, -1)

    def join(top, bottom):
        upper = jnp.concatenate(top, axis=2).reshape(rows, -1)
        lower = jnp.concatenate(bottom, axis=2).reshape(rows, -1)
        return jnp.concatenate([upper, lower], axis=0)

    return join([er, ei], [-ei, er])


def spectrum_kernel(
    slot_ref, own_re, own_im, far_re, far_im, col_a, row_re, row_im, *rest
):
    out_ref = rest[-1]
    fp = jnp.float32
    bf = jnp.bfloat16
    a_re = own_re[0, 0].astype(fp)
    a_im = own_im[0, 0].astype(fp)
    b_re = far_re[0, 0].astype(fp)
    b_im = far_im[0, 0].astype(fp)
    z_re = (a_re * b_re + a_im * b_im).astype(bf)
    z_im = (a_im * b_re - a_re * b_im).astype(bf)
    n = z_re.shape[1]
    y = (
        jnp.dot(z_re, col_a[:n, :], preferred_element_type=fp)
        + jnp.dot(z_im, col_a[n:, :], preferred_element_type=fp)
    ).astype(bf)
    first = jnp.dot(row_re[...], y, preferred_element_type=fp)
    second = jnp.dot(row_im[...], y, preferred_element_type=fp)
    blocks, groups, _, rows_per, lanes = out_ref.shape
    lane = lax.broadcasted_iota(jnp.int32, (first.shape[0], lanes), 1)
    for block in range(blocks):
        cut = slice(block * lanes, (block + 1) * lanes)
        swapped = pltpu.roll(second[:, cut], lanes // 2, 1)
        swapped = jnp.where(lane < lanes // 2, -swapped, swapped)
        spec = (first[:, cut] + swapped).astype(bf)
        out_ref[block, :, 0, :, :] = spec.reshape(groups, rows_per, lanes)


def spectra(slots, own_re, own_im, far_re, far_im, col_a, row_re, row_im, blocks, groups, after):
    waves, _, rows, cols = own_re.shape
    lanes = 2 * cols // blocks
    rows_per = rows // groups
    field = pl.BlockSpec((1, 1, rows, cols), lambda i, sl: (i, 0, 0, 0))
    partner = pl.BlockSpec((1, 1, rows, cols), lambda i, sl: (sl[i], 0, 0, 0))
    whole_col = pl.BlockSpec((2 * cols, 2 * cols), lambda i, sl: (0, 0))
    whole_row = pl.BlockSpec((rows, rows), lambda i, sl: (0, 0))
    flops = waves * (2 * rows * (2 * cols) * (2 * cols) + 2 * 2 * rows * rows * (2 * cols))
    return pl.pallas_call(
        spectrum_kernel,
        out_shape=jax.ShapeDtypeStruct((blocks, groups, waves, rows_per, lanes), jnp.bfloat16),
        grid_spec=pltpu.PrefetchScalarGridSpec(
            num_scalar_prefetch=1,
            grid=(waves,),
            in_specs=[field, field, partner, partner, whole_col, whole_row, whole_row]
            + [pl.BlockSpec(memory_space=pl.ANY)] * len(after),
            out_specs=pl.BlockSpec(
                (blocks, groups, 1, rows_per, lanes), lambda i, sl: (0, 0, i, 0, 0)
            ),
        ),
        compiler_params=pltpu.CompilerParams(vmem_limit_bytes=60 * 1024 * 1024),
        cost_estimate=pl.CostEstimate(
            flops=flops, transcendentals=0, bytes_accessed=waves * rows * cols * 12 + 12 * cols * cols
        ),
    )(slots, own_re, own_im, far_re, far_im, col_a, row_re, row_im, *after)


def shards(hologram_real, hologram_imaginary, pair_slot, kernel_real, kernel_imaginary):
    fp = jnp.float32
    wave_devices = lax.axis_size("wave")
    angle_devices = lax.axis_size("angle")
    local_waves, local_angles, row_count, col_count = hologram_real.shape
    section_count = pair_slot.shape[0]
    depth_count = kernel_real.shape[3]
    row_real, row_imag = dft_tables(row_count)
    col_real, col_imag = dft_tables(col_count)
    col_a = column_tables(col_real, col_imag, wave_devices)

    def all_weights(kernel_part):
        block = kernel_part.reshape(
            wave_devices, local_waves, section_count, angle_devices, depth_count
        )
        return jnp.transpose(block, (2, 0, 3, 1, 4)).reshape(
            section_count, wave_devices * angle_devices, local_waves, depth_count
        )

    k_re = all_weights(kernel_real)
    k_im = all_weights(kernel_imaginary)
    volume = None
    received = [
        from_partner((hologram_real, hologram_imaginary), "wave", section_number)
        for section_number in range(section_count)
    ]
    for section_number in range(section_count):
        got_real, got_imag = received[section_number]
        after = [a for other, got in enumerate(received) if other != section_number for a in got]
        send = spectra(
            pair_slot[section_number],
            hologram_real,
            hologram_imaginary,
            got_real,
            got_imag,
            col_a,
            row_real,
            row_imag,
            wave_devices,
            angle_devices,
            after,
        )
        send = send.reshape(wave_devices * angle_devices, *send.shape[2:])
        got = lax.all_to_all(send, ("wave", "angle"), 0, 0, tiled=True)
        got = with_layout_constraint(got, Layout(tuple(range(got.ndim))))
        kr = k_re[section_number]
        ki = k_im[section_number]
        w_first = jnp.stack([kr, ki], axis=2).reshape(kr.shape[0], kr.shape[1], -1)
        w_second = jnp.stack([-ki, kr], axis=2).reshape(kr.shape[0], kr.shape[1], -1)
        t_first = jnp.einsum("swrn,swx->rnx", got, w_first, preferred_element_type=fp)
        t_second = jnp.einsum("swrn,swx->rnx", got, w_second, preferred_element_type=fp)
        half = got.shape[3] // 2
        part = t_first[:, :half] + t_second[:, half:]
        volume = part if volume is None else volume + part
    return (volume[:, :, :depth_count], volume[:, :, depth_count:])


def solution(mesh):
    return jax.shard_map(
        shards,
        mesh=mesh,
        in_specs=(
            P("wave", "angle", None, None),
            P("wave", "angle", None, None),
            P(None, "wave"),
            P(),
            P(),
        ),
        out_specs=(P("angle", "wave", None), P("angle", "wave", None)),
        check_vma=False,
    )
```

```python
import functools
import math

import jax
import jax.numpy as jnp
from jax import lax
from jax.experimental import pallas as pl
from jax.experimental.layout import Layout, with_layout_constraint
from jax.experimental.pallas import tpu as pltpu
from jax.sharding import PartitionSpec as P


def from_partner(block, axis, bit):
    count = lax.axis_size(axis)
    route = []
    for low in range(count):
        high = low | 1 << bit
        if high != low and high < count:
            route += [(low, high), (high, low)]
    return lax.ppermute(block, axis, route)


def dft_tables(length):
    counter = jnp.arange(length, dtype=jnp.int32)
    product = counter[:, None] * counter[None, :] % length
    phase = product.astype(jnp.float32) * (2.0 * math.pi / length)
    factor = 1.0 / math.sqrt(length)
    return (
        (jnp.cos(phase) * factor).astype(jnp.bfloat16),
        (-jnp.sin(phase) * factor).astype(jnp.bfloat16),
    )


def column_tables(table_real, table_imag, blocks):
    rows = table_real.shape[0]
    er = table_real.reshape(rows, blocks, 1, -1)
    ei = table_imag.reshape(rows, blocks, 1, -1)

    def join(top, bottom):
        upper = jnp.concatenate(top, axis=2).reshape(rows, -1)
        lower = jnp.concatenate(bottom, axis=2).reshape(rows, -1)
        return jnp.concatenate([upper, lower], axis=0)

    return join([er, ei], [-ei, er])


def spectrum_kernel(
    slot_ref, own_re, own_im, far_re, far_im, col_a, row_re, row_im, *rest
):
    out_ref = rest[-1]
    fp = jnp.float32
    bf = jnp.bfloat16
    a_re = own_re[0, 0].astype(fp)
    a_im = own_im[0, 0].astype(fp)
    b_re = far_re[0, 0].astype(fp)
    b_im = far_im[0, 0].astype(fp)
    z_re = (a_re * b_re + a_im * b_im).astype(bf)
    z_im = (a_im * b_re - a_re * b_im).astype(bf)
    n = z_re.shape[1]
    y = (
        jnp.dot(z_re, col_a[:n, :], preferred_element_type=fp)
        + jnp.dot(z_im, col_a[n:, :], preferred_element_type=fp)
    ).astype(bf)
    first = jnp.dot(row_re[...], y, preferred_element_type=fp)
    second = jnp.dot(row_im[...], y, preferred_element_type=fp)
    blocks, groups, _, rows_per, lanes = out_ref.shape
    lane = lax.broadcasted_iota(jnp.int32, (first.shape[0], lanes), 1)
    for block in range(blocks):
        cut = slice(block * lanes, (block + 1) * lanes)
        swapped = pltpu.roll(second[:, cut], lanes // 2, 1)
        swapped = jnp.where(lane < lanes // 2, -swapped, swapped)
        spec = (first[:, cut] + swapped).astype(bf)
        out_ref[block, :, 0, :, :] = spec.reshape(groups, rows_per, lanes)


def spectra(slots, own_re, own_im, far_re, far_im, col_a, row_re, row_im, blocks, groups, after):
    waves, _, rows, cols = own_re.shape
    lanes = 2 * cols // blocks
    rows_per = rows // groups
    field = pl.BlockSpec((1, 1, rows, cols), lambda i, sl: (i, 0, 0, 0))
    partner = pl.BlockSpec((1, 1, rows, cols), lambda i, sl: (sl[i], 0, 0, 0))
    whole_col = pl.BlockSpec((2 * cols, 2 * cols), lambda i, sl: (0, 0))
    whole_row = pl.BlockSpec((rows, rows), lambda i, sl: (0, 0))
    flops = waves * (2 * rows * (2 * cols) * (2 * cols) + 2 * 2 * rows * rows * (2 * cols))
    return pl.pallas_call(
        spectrum_kernel,
        out_shape=jax.ShapeDtypeStruct((blocks, groups, waves, rows_per, lanes), jnp.bfloat16),
        grid_spec=pltpu.PrefetchScalarGridSpec(
            num_scalar_prefetch=1,
            grid=(waves,),
            in_specs=[field, field, partner, partner, whole_col, whole_row, whole_row]
            + [pl.BlockSpec(memory_space=pl.ANY)] * len(after),
            out_specs=pl.BlockSpec(
                (blocks, groups, 1, rows_per, lanes), lambda i, sl: (0, 0, i, 0, 0)
            ),
        ),
        compiler_params=pltpu.CompilerParams(vmem_limit_bytes=60 * 1024 * 1024),
        cost_estimate=pl.CostEstimate(
            flops=flops, transcendentals=0, bytes_accessed=waves * rows * cols * 12 + 12 * cols * cols
        ),
    )(slots, own_re, own_im, far_re, far_im, col_a, row_re, row_im, *after)


def shards(hologram_real, hologram_imaginary, pair_slot, kernel_real, kernel_imaginary):
    fp = jnp.float32
    wave_devices = lax.axis_size("wave")
    angle_devices = lax.axis_size("angle")
    local_waves, local_angles, row_count, col_count = hologram_real.shape
    section_count = pair_slot.shape[0]
    depth_count = kernel_real.shape[3]
    row_real, row_imag = dft_tables(row_count)
    col_real, col_imag = dft_tables(col_count)
    col_a = column_tables(col_real, col_imag, wave_devices)

    def all_weights(kernel_part):
        block = kernel_part.reshape(
            wave_devices, local_waves, section_count, angle_devices, depth_count
        )
        return jnp.transpose(block, (2, 0, 3, 1, 4)).reshape(
            section_count, wave_devices * angle_devices, local_waves, depth_count
        )

    k_re = all_weights(kernel_real)
    k_im = all_weights(kernel_imaginary)
    volume = None
    received = [
        from_partner((hologram_real, hologram_imaginary), "wave", section_number)
        for section_number in range(section_count)
    ]
    for section_number in range(section_count):
        got_real, got_imag = received[section_number]
        after = [a for other, got in enumerate(received) if other != section_number for a in got]
        send = spectra(
            pair_slot[section_number],
            hologram_real,
            hologram_imaginary,
            got_real,
            got_imag,
            col_a,
            row_real,
            row_imag,
            wave_devices,
            angle_devices,
            after,
        )
        send = send.reshape(wave_devices * angle_devices, *send.shape[2:])
        got = lax.all_to_all(send, ("wave", "angle"), 0, 0, tiled=True)
        got = with_layout_constraint(got, Layout(tuple(range(got.ndim))))
        kr = k_re[section_number]
        ki = k_im[section_number]
        w_first = jnp.stack([kr, ki], axis=2).reshape(kr.shape[0], kr.shape[1], -1)
        w_second = jnp.stack([-ki, kr], axis=2).reshape(kr.shape[0], kr.shape[1], -1)
        both = jnp.concatenate([w_first, w_second], axis=2)
        t = jnp.einsum("swrn,swx->rnx", got, both, preferred_element_type=fp)
        half = got.shape[3] // 2
        width = w_first.shape[2]
        part = t[:, :half, :width] + t[:, half:, width:]
        volume = part if volume is None else volume + part
    return (volume[:, :, :depth_count], volume[:, :, depth_count:])


def solution(mesh):
    return jax.shard_map(
        shards,
        mesh=mesh,
        in_specs=(
            P("wave", "angle", None, None),
            P("wave", "angle", None, None),
            P(None, "wave"),
            P(),
            P(),
        ),
        out_specs=(P("angle", "wave", None), P("angle", "wave", None)),
        check_vma=False,
    )
```

```python
import functools
import math

import jax
import jax.numpy as jnp
from jax import lax
from jax.experimental import pallas as pl
from jax.experimental.layout import Layout, with_layout_constraint
from jax.experimental.pallas import tpu as pltpu
from jax.sharding import PartitionSpec as P


def from_partner(block, axis, bit):
    count = lax.axis_size(axis)
    route = []
    for low in range(count):
        high = low | 1 << bit
        if high != low and high < count:
            route += [(low, high), (high, low)]
    return lax.ppermute(block, axis, route)


def dft_tables(length):
    counter = jnp.arange(length, dtype=jnp.int32)
    product = counter[:, None] * counter[None, :] % length
    phase = product.astype(jnp.float32) * (2.0 * math.pi / length)
    factor = 1.0 / math.sqrt(length)
    return (
        (jnp.cos(phase) * factor).astype(jnp.bfloat16),
        (-jnp.sin(phase) * factor).astype(jnp.bfloat16),
    )


def column_tables(table_real, table_imag, blocks):
    rows = table_real.shape[0]
    er = table_real.reshape(rows, blocks, 1, -1)
    ei = table_imag.reshape(rows, blocks, 1, -1)

    def join(top, bottom):
        upper = jnp.concatenate(top, axis=2).reshape(rows, -1)
        lower = jnp.concatenate(bottom, axis=2).reshape(rows, -1)
        return jnp.concatenate([upper, lower], axis=0)

    return join([er, ei], [-ei, er])


def spectrum_kernel(
    slot_ref, own_re, own_im, far_re, far_im, col_a, row_re, row_im, *rest
):
    out_ref = rest[-1]
    fp = jnp.float32
    bf = jnp.bfloat16
    a_re = own_re[0, 0].astype(fp)
    a_im = own_im[0, 0].astype(fp)
    b_re = far_re[0, 0].astype(fp)
    b_im = far_im[0, 0].astype(fp)
    z_re = (a_re * b_re + a_im * b_im).astype(bf)
    z_im = (a_im * b_re - a_re * b_im).astype(bf)
    z = jnp.concatenate([z_re, z_im], axis=1)
    y = jnp.dot(z, col_a[...], preferred_element_type=fp).astype(bf)
    first = jnp.dot(row_re[...], y, preferred_element_type=fp)
    second = jnp.dot(row_im[...], y, preferred_element_type=fp)
    blocks, groups, _, rows_per, lanes = out_ref.shape
    lane = lax.broadcasted_iota(jnp.int32, (first.shape[0], lanes), 1)
    for block in range(blocks):
        cut = slice(block * lanes, (block + 1) * lanes)
        swapped = pltpu.roll(second[:, cut], lanes // 2, 1)
        swapped = jnp.where(lane < lanes // 2, -swapped, swapped)
        spec = (first[:, cut] + swapped).astype(bf)
        out_ref[block, :, 0, :, :] = spec.reshape(groups, rows_per, lanes)


def spectra(slots, own_re, own_im, far_re, far_im, col_a, row_re, row_im, blocks, groups, after):
    waves, _, rows, cols = own_re.shape
    lanes = 2 * cols // blocks
    rows_per = rows // groups
    field = pl.BlockSpec((1, 1, rows, cols), lambda i, sl: (i, 0, 0, 0))
    partner = pl.BlockSpec((1, 1, rows, cols), lambda i, sl: (sl[i], 0, 0, 0))
    whole_col = pl.BlockSpec((2 * cols, 2 * cols), lambda i, sl: (0, 0))
    whole_row = pl.BlockSpec((rows, rows), lambda i, sl: (0, 0))
    flops = waves * (2 * rows * (2 * cols) * (2 * cols) + 2 * 2 * rows * rows * (2 * cols))
    return pl.pallas_call(
        spectrum_kernel,
        out_shape=jax.ShapeDtypeStruct((blocks, groups, waves, rows_per, lanes), jnp.bfloat16),
        grid_spec=pltpu.PrefetchScalarGridSpec(
            num_scalar_prefetch=1,
            grid=(waves,),
            in_specs=[field, field, partner, partner, whole_col, whole_row, whole_row]
            + [pl.BlockSpec(memory_space=pl.ANY)] * len(after),
            out_specs=pl.BlockSpec(
                (blocks, groups, 1, rows_per, lanes), lambda i, sl: (0, 0, i, 0, 0)
            ),
        ),
        compiler_params=pltpu.CompilerParams(vmem_limit_bytes=60 * 1024 * 1024),
        cost_estimate=pl.CostEstimate(
            flops=flops, transcendentals=0, bytes_accessed=waves * rows * cols * 12 + 12 * cols * cols
        ),
    )(slots, own_re, own_im, far_re, far_im, col_a, row_re, row_im, *after)


def shards(hologram_real, hologram_imaginary, pair_slot, kernel_real, kernel_imaginary):
    fp = jnp.float32
    wave_devices = lax.axis_size("wave")
    angle_devices = lax.axis_size("angle")
    local_waves, local_angles, row_count, col_count = hologram_real.shape
    section_count = pair_slot.shape[0]
    depth_count = kernel_real.shape[3]
    row_real, row_imag = dft_tables(row_count)
    col_real, col_imag = dft_tables(col_count)
    col_a = column_tables(col_real, col_imag, wave_devices)

    def all_weights(kernel_part):
        block = kernel_part.reshape(
            wave_devices, local_waves, section_count, angle_devices, depth_count
        )
        return jnp.transpose(block, (2, 0, 3, 1, 4)).reshape(
            section_count, wave_devices * angle_devices, local_waves, depth_count
        )

    k_re = all_weights(kernel_real)
    k_im = all_weights(kernel_imaginary)
    volume = None
    received = [
        from_partner((hologram_real, hologram_imaginary), "wave", section_number)
        for section_number in range(section_count)
    ]
    for section_number in range(section_count):
        got_real, got_imag = received[section_number]
        after = [a for other, got in enumerate(received) if other != section_number for a in got]
        send = spectra(
            pair_slot[section_number],
            hologram_real,
            hologram_imaginary,
            got_real,
            got_imag,
            col_a,
            row_real,
            row_imag,
            wave_devices,
            angle_devices,
            after,
        )
        send = send.reshape(wave_devices * angle_devices, *send.shape[2:])
        got = lax.all_to_all(send, ("wave", "angle"), 0, 0, tiled=True)
        got = with_layout_constraint(got, Layout(tuple(range(got.ndim))))
        kr = k_re[section_number]
        ki = k_im[section_number]
        w_first = jnp.stack([kr, ki], axis=2).reshape(kr.shape[0], kr.shape[1], -1)
        w_second = jnp.stack([-ki, kr], axis=2).reshape(kr.shape[0], kr.shape[1], -1)
        both = jnp.concatenate([w_first, w_second], axis=2)
        t = jnp.einsum("swrn,swx->rnx", got, both, preferred_element_type=fp)
        half = got.shape[3] // 2
        width = w_first.shape[2]
        part = t[:, :half, :width] + t[:, half:, width:]
        volume = part if volume is None else volume + part
    return (volume[:, :, :depth_count], volume[:, :, depth_count:])


def solution(mesh):
    return jax.shard_map(
        shards,
        mesh=mesh,
        in_specs=(
            P("wave", "angle", None, None),
            P("wave", "angle", None, None),
            P(None, "wave"),
            P(),
            P(),
        ),
        out_specs=(P("angle", "wave", None), P("angle", "wave", None)),
        check_vma=False,
    )
```

```python
import functools
import math

import jax
import jax.numpy as jnp
from jax import lax
from jax.experimental import pallas as pl
from jax.experimental.layout import Layout, with_layout_constraint
from jax.experimental.pallas import tpu as pltpu
from jax.sharding import PartitionSpec as P


def from_partner(block, axis, bit):
    count = lax.axis_size(axis)
    route = []
    for low in range(count):
        high = low | 1 << bit
        if high != low and high < count:
            route += [(low, high), (high, low)]
    return lax.ppermute(block, axis, route)


def dft_tables(length):
    counter = jnp.arange(length, dtype=jnp.int32)
    product = counter[:, None] * counter[None, :] % length
    phase = product.astype(jnp.float32) * (2.0 * math.pi / length)
    factor = 1.0 / math.sqrt(length)
    return (
        (jnp.cos(phase) * factor).astype(jnp.bfloat16),
        (-jnp.sin(phase) * factor).astype(jnp.bfloat16),
    )


def column_tables(table_real, table_imag, blocks):
    rows = table_real.shape[0]
    er = table_real.reshape(rows, blocks, 1, -1)
    ei = table_imag.reshape(rows, blocks, 1, -1)

    def join(top, bottom):
        upper = jnp.concatenate(top, axis=2).reshape(rows, -1)
        lower = jnp.concatenate(bottom, axis=2).reshape(rows, -1)
        return jnp.concatenate([upper, lower], axis=0)

    return join([er, ei], [-ei, er])


def spectrum_kernel(slot_ref, own_re, own_im, far_re, far_im, col_a, row_re, row_im, *rest):
    fp = jnp.float32
    bf = jnp.bfloat16
    out_ref = rest[-1]
    final = len(out_ref.shape) == 5
    a_re = own_re[0, 0].astype(fp)
    a_im = own_im[0, 0].astype(fp)
    b_re = far_re[0, 0].astype(fp)
    b_im = far_im[0, 0].astype(fp)
    z_re = (a_re * b_re + a_im * b_im).astype(bf)
    z_im = (a_im * b_re - a_re * b_im).astype(bf)
    z = jnp.concatenate([z_re, z_im], axis=1)
    y = jnp.dot(z, col_a[...], preferred_element_type=fp).astype(bf)
    first = jnp.dot(row_re[...], y, preferred_element_type=fp)
    second = jnp.dot(row_im[...], y, preferred_element_type=fp)
    lanes = out_ref.shape[-1] if final else 128
    blocks = first.shape[1] // lanes
    lane = lax.broadcasted_iota(jnp.int32, (first.shape[0], lanes), 1)
    for block in range(blocks):
        cut = slice(block * lanes, (block + 1) * lanes)
        swapped = pltpu.roll(second[:, cut], lanes // 2, 1)
        swapped = jnp.where(lane < lanes // 2, -swapped, swapped)
        total = first[:, cut] + swapped
        if final:
            total = (rest[-2][0, :, cut] + total).astype(bf)
            _, groups, _, rows_per, _ = out_ref.shape
            out_ref[block, :, 0, :, :] = total.reshape(groups, rows_per, lanes)
        else:
            out_ref[0, :, cut] = total


def spectra(slots, own_re, own_im, far_re, far_im, tables, half, blocks, groups, after, partial):
    col_a, row_re, row_im = tables
    waves, _, rows, cols = own_re.shape
    h = far_re.shape[2]
    lanes = 2 * cols // blocks
    rows_per = rows // groups
    field = pl.BlockSpec((1, 1, h, cols), lambda i, sl: (i, 0, half, 0))
    partner = pl.BlockSpec((1, 1, h, cols), lambda i, sl: (sl[i], 0, 0, 0))
    whole_col = pl.BlockSpec((2 * cols, 2 * cols), lambda i, sl: (0, 0))
    row_part = pl.BlockSpec((rows, h), lambda i, sl: (0, half))
    per_wave = pl.BlockSpec((1, rows, 2 * cols), lambda i, sl: (i, 0, 0))
    flops = waves * (2 * h * (2 * cols) * (2 * cols) + 2 * 2 * rows * h * (2 * cols))
    in_specs = [field, field, partner, partner, whole_col, row_part, row_part]
    in_specs += [pl.BlockSpec(memory_space=pl.ANY)] * len(after)
    extra = list(after)
    if partial is None:
        out_shape = jax.ShapeDtypeStruct((waves, rows, 2 * cols), jnp.float32)
        out_spec = per_wave
    else:
        in_specs.append(per_wave)
        extra.append(partial)
        out_shape = jax.ShapeDtypeStruct((blocks, groups, waves, rows_per, lanes), jnp.bfloat16)
        out_spec = pl.BlockSpec(
            (blocks, groups, 1, rows_per, lanes), lambda i, sl: (0, 0, i, 0, 0)
        )
    return pl.pallas_call(
        spectrum_kernel,
        out_shape=out_shape,
        grid_spec=pltpu.PrefetchScalarGridSpec(
            num_scalar_prefetch=1,
            grid=(waves,),
            in_specs=in_specs,
            out_specs=out_spec,
        ),
        compiler_params=pltpu.CompilerParams(vmem_limit_bytes=60 * 1024 * 1024),
        cost_estimate=pl.CostEstimate(
            flops=flops, transcendentals=0, bytes_accessed=waves * rows * cols * 14 + 8 * cols * cols
        ),
    )(slots, own_re, own_im, far_re, far_im, col_a, row_re, row_im, *extra)


def shards(hologram_real, hologram_imaginary, pair_slot, kernel_real, kernel_imaginary):
    fp = jnp.float32
    wave_devices = lax.axis_size("wave")
    angle_devices = lax.axis_size("angle")
    local_waves, local_angles, row_count, col_count = hologram_real.shape
    section_count = pair_slot.shape[0]
    depth_count = kernel_real.shape[3]
    row_real, row_imag = dft_tables(row_count)
    col_real, col_imag = dft_tables(col_count)
    col_a = column_tables(col_real, col_imag, wave_devices)

    def all_weights(kernel_part):
        block = kernel_part.reshape(
            wave_devices, local_waves, section_count, angle_devices, depth_count
        )
        return jnp.transpose(block, (2, 0, 3, 1, 4)).reshape(
            section_count, wave_devices * angle_devices, local_waves, depth_count
        )

    k_re = all_weights(kernel_real)
    k_im = all_weights(kernel_imaginary)
    volume = None
    halves = 2
    h = row_count // halves
    received = [
        [
            from_partner(
                (hologram_real[:, :, c * h : (c + 1) * h], hologram_imaginary[:, :, c * h : (c + 1) * h]),
                "wave",
                section_number,
            )
            for c in range(halves)
        ]
        for section_number in range(section_count)
    ]
    tables = (col_a, row_real, row_imag)
    volume = None
    for section_number in range(section_count):
        partial = None
        for c in range(halves):
            got_real, got_imag = received[section_number][c]
            after = [
                a for other in range(section_count) if other != section_number for a in received[other][c]
            ]
            partial = spectra(
                pair_slot[section_number],
                hologram_real,
                hologram_imaginary,
                got_real,
                got_imag,
                tables,
                c,
                wave_devices,
                angle_devices,
                after,
                partial,
            )
        send = partial
        send = send.reshape(wave_devices * angle_devices, *send.shape[2:])
        got = lax.all_to_all(send, ("wave", "angle"), 0, 0, tiled=True)
        got = with_layout_constraint(got, Layout(tuple(range(got.ndim))))
        kr = k_re[section_number]
        ki = k_im[section_number]
        w_first = jnp.stack([kr, ki], axis=2).reshape(kr.shape[0], kr.shape[1], -1)
        w_second = jnp.stack([-ki, kr], axis=2).reshape(kr.shape[0], kr.shape[1], -1)
        both = jnp.concatenate([w_first, w_second], axis=2)
        t = jnp.einsum("swrn,swx->rnx", got, both, preferred_element_type=fp)
        half = got.shape[3] // 2
        width = w_first.shape[2]
        part = t[:, :half, :width] + t[:, half:, width:]
        volume = part if volume is None else volume + part
    return (volume[:, :, :depth_count], volume[:, :, depth_count:])


def solution(mesh):
    return jax.shard_map(
        shards,
        mesh=mesh,
        in_specs=(
            P("wave", "angle", None, None),
            P("wave", "angle", None, None),
            P(None, "wave"),
            P(),
            P(),
        ),
        out_specs=(P("angle", "wave", None), P("angle", "wave", None)),
        check_vma=False,
    )
```

```python
import functools
import math

import jax
import jax.numpy as jnp
from jax import lax
from jax.experimental import pallas as pl
from jax.experimental.layout import Layout, with_layout_constraint
from jax.experimental.pallas import tpu as pltpu
from jax.sharding import PartitionSpec as P


def from_partner(block, axis, bit):
    count = lax.axis_size(axis)
    route = []
    for low in range(count):
        high = low | 1 << bit
        if high != low and high < count:
            route += [(low, high), (high, low)]
    return lax.ppermute(block, axis, route)


def dft_tables(length):
    counter = jnp.arange(length, dtype=jnp.int32)
    product = counter[:, None] * counter[None, :] % length
    phase = product.astype(jnp.float32) * (2.0 * math.pi / length)
    factor = 1.0 / math.sqrt(length)
    return (
        (jnp.cos(phase) * factor).astype(jnp.bfloat16),
        (-jnp.sin(phase) * factor).astype(jnp.bfloat16),
    )


def column_tables(table_real, table_imag, blocks):
    rows = table_real.shape[0]
    er = table_real.reshape(rows, blocks, 1, -1)
    ei = table_imag.reshape(rows, blocks, 1, -1)

    def join(top, bottom):
        upper = jnp.concatenate(top, axis=2).reshape(rows, -1)
        lower = jnp.concatenate(bottom, axis=2).reshape(rows, -1)
        return jnp.concatenate([upper, lower], axis=0)

    return join([er, ei], [-ei, er])


def spectrum_kernel(
    slot_ref, own_re, own_im, far_re, far_im, col_a, row_re, row_im, *rest
):
    out_ref = rest[-1]
    fp = jnp.float32
    bf = jnp.bfloat16
    a_re = own_re[0, 0].astype(fp)
    a_im = own_im[0, 0].astype(fp)
    b_re = far_re[0, 0].astype(fp)
    b_im = far_im[0, 0].astype(fp)
    z_re = (a_re * b_re + a_im * b_im).astype(bf)
    z_im = (a_im * b_re - a_re * b_im).astype(bf)
    z = jnp.concatenate([z_re, z_im], axis=1)
    y = jnp.dot(z, col_a[...], preferred_element_type=fp).astype(bf)
    first = jnp.dot(row_re[...], y, preferred_element_type=fp)
    second = jnp.dot(row_im[...], y, preferred_element_type=fp)
    blocks, groups, _, rows_per, lanes = out_ref.shape
    lane = lax.broadcasted_iota(jnp.int32, (first.shape[0], lanes), 1)
    for block in range(blocks):
        cut = slice(block * lanes, (block + 1) * lanes)
        swapped = pltpu.roll(second[:, cut], lanes // 2, 1)
        swapped = jnp.where(lane < lanes // 2, -swapped, swapped)
        spec = (first[:, cut] + swapped).astype(bf)
        out_ref[block, :, 0, :, :] = spec.reshape(groups, rows_per, lanes)


def spectra(slots, own_re, own_im, far_re, far_im, tables, shape, first, waves, slot, after, into):
    col_a, row_re, row_im = tables
    _, _, rows, cols = own_re.shape
    blocks, groups, _, rows_per, lanes = shape
    field = pl.BlockSpec((1, 1, rows, cols), lambda i, sl: (first + i, 0, 0, 0))
    partner = pl.BlockSpec((1, 1, rows, cols), lambda i, sl: (sl[first + i], 0, 0, 0))
    whole_col = pl.BlockSpec((2 * cols, 2 * cols), lambda i, sl: (0, 0))
    whole_row = pl.BlockSpec((rows, rows), lambda i, sl: (0, 0))
    flops = waves * (2 * rows * (2 * cols) * (2 * cols) + 2 * 2 * rows * rows * (2 * cols))
    extra = list(after) + ([] if into is None else [into])
    return pl.pallas_call(
        spectrum_kernel,
        out_shape=jax.ShapeDtypeStruct(shape, jnp.bfloat16),
        grid_spec=pltpu.PrefetchScalarGridSpec(
            num_scalar_prefetch=1,
            grid=(waves,),
            in_specs=[field, field, partner, partner, whole_col, whole_row, whole_row]
            + [pl.BlockSpec(memory_space=pl.ANY)] * len(extra),
            out_specs=pl.BlockSpec(
                (blocks, groups, 1, rows_per, lanes), lambda i, sl: (0, 0, slot + i, 0, 0)
            ),
        ),
        input_output_aliases={} if into is None else {8 + len(after): 0},
        compiler_params=pltpu.CompilerParams(vmem_limit_bytes=60 * 1024 * 1024),
        cost_estimate=pl.CostEstimate(
            flops=flops, transcendentals=0, bytes_accessed=waves * rows * cols * 12 + 12 * cols * cols
        ),
    )(slots, own_re, own_im, far_re, far_im, col_a, row_re, row_im, *extra)


def shards(hologram_real, hologram_imaginary, pair_slot, kernel_real, kernel_imaginary):
    fp = jnp.float32
    wave_devices = lax.axis_size("wave")
    angle_devices = lax.axis_size("angle")
    local_waves, local_angles, row_count, col_count = hologram_real.shape
    section_count = pair_slot.shape[0]
    depth_count = kernel_real.shape[3]
    row_real, row_imag = dft_tables(row_count)
    col_real, col_imag = dft_tables(col_count)
    tables = (column_tables(col_real, col_imag, wave_devices), row_real, row_imag)
    lanes = 2 * col_count // wave_devices
    rows_per = row_count // angle_devices

    def all_weights(kernel_part):
        block = kernel_part.reshape(
            wave_devices, local_waves, section_count, angle_devices, depth_count
        )
        return jnp.transpose(block, (0, 3, 2, 1, 4)).reshape(
            wave_devices * angle_devices, section_count * local_waves, depth_count
        )

    k_re = all_weights(kernel_real)
    k_im = all_weights(kernel_imaginary)
    received = [
        from_partner((hologram_real, hologram_imaginary), "wave", section_number)
        for section_number in range(section_count)
    ]
    total = section_count * local_waves
    small = local_waves // 2
    split = [(total - small, total), (0, total - small)]
    volume = None
    for low, high in split:
        shape = (wave_devices, angle_devices, high - low, rows_per, lanes)
        send = None
        for section_number in range(section_count):
            lo = max(low, section_number * local_waves)
            hi = min(high, (section_number + 1) * local_waves)
            if lo >= hi:
                continue
            got_real, got_imag = received[section_number]
            after = [a for other, got in enumerate(received) if other != section_number for a in got]
            send = spectra(
                pair_slot[section_number],
                hologram_real,
                hologram_imaginary,
                got_real,
                got_imag,
                tables,
                shape,
                lo - section_number * local_waves,
                hi - lo,
                lo - low,
                after,
                send,
            )
        send = send.reshape(wave_devices * angle_devices, *send.shape[2:])
        got = lax.all_to_all(send, ("wave", "angle"), 0, 0, tiled=True)
        got = with_layout_constraint(got, Layout(tuple(range(got.ndim))))
        kr = k_re[:, low:high]
        ki = k_im[:, low:high]
        w_first = jnp.stack([kr, ki], axis=2).reshape(kr.shape[0], kr.shape[1], -1)
        w_second = jnp.stack([-ki, kr], axis=2).reshape(kr.shape[0], kr.shape[1], -1)
        both = jnp.concatenate([w_first, w_second], axis=2)
        t = jnp.einsum("swrn,swx->rnx", got, both, preferred_element_type=fp)
        half = got.shape[3] // 2
        width = w_first.shape[2]
        part = t[:, :half, :width] + t[:, half:, width:]
        volume = part if volume is None else volume + part
    return (volume[:, :, :depth_count], volume[:, :, depth_count:])


def solution(mesh):
    return jax.shard_map(
        shards,
        mesh=mesh,
        in_specs=(
            P("wave", "angle", None, None),
            P("wave", "angle", None, None),
            P(None, "wave"),
            P(),
            P(),
        ),
        out_specs=(P("angle", "wave", None), P("angle", "wave", None)),
        check_vma=False,
    )
```

```python
import functools
import math

import jax
import jax.numpy as jnp
from jax import lax
from jax.experimental import pallas as pl
from jax.experimental.layout import Layout, with_layout_constraint
from jax.experimental.pallas import tpu as pltpu
from jax.sharding import PartitionSpec as P


def from_partner(block, axis, bit):
    count = lax.axis_size(axis)
    route = []
    for low in range(count):
        high = low | 1 << bit
        if high != low and high < count:
            route += [(low, high), (high, low)]
    return lax.ppermute(block, axis, route)


def dft_tables(length):
    counter = jnp.arange(length, dtype=jnp.int32)
    product = counter[:, None] * counter[None, :] % length
    phase = product.astype(jnp.float32) * (2.0 * math.pi / length)
    factor = 1.0 / math.sqrt(length)
    return (
        (jnp.cos(phase) * factor).astype(jnp.bfloat16),
        (-jnp.sin(phase) * factor).astype(jnp.bfloat16),
    )


def column_tables(table_real, table_imag, blocks):
    rows = table_real.shape[0]
    er = table_real.reshape(rows, blocks, 1, -1)
    ei = table_imag.reshape(rows, blocks, 1, -1)

    def join(top, bottom):
        upper = jnp.concatenate(top, axis=2).reshape(rows, -1)
        lower = jnp.concatenate(bottom, axis=2).reshape(rows, -1)
        return jnp.concatenate([upper, lower], axis=0)

    return join([er, ei], [-ei, er])


def spectrum_kernel(
    slot_ref, own_re, own_im, far_re, far_im, col_a, row_re, row_im, *rest
):
    out_ref = rest[-1]
    fp = jnp.float32
    bf = jnp.bfloat16
    a_re = own_re[0, 0].astype(fp)
    a_im = own_im[0, 0].astype(fp)
    b_re = far_re[0, 0].astype(fp)
    b_im = far_im[0, 0].astype(fp)
    z_re = (a_re * b_re + a_im * b_im).astype(bf)
    z_im = (a_im * b_re - a_re * b_im).astype(bf)
    z = jnp.concatenate([z_re, z_im], axis=1)
    y = jnp.dot(z, col_a[...], preferred_element_type=fp).astype(bf)
    first = jnp.dot(row_re[...], y, preferred_element_type=fp)
    second = jnp.dot(row_im[...], y, preferred_element_type=fp)
    blocks, groups, _, rows_per, lanes = out_ref.shape
    lane = lax.broadcasted_iota(jnp.int32, (first.shape[0], lanes), 1)
    for block in range(blocks):
        cut = slice(block * lanes, (block + 1) * lanes)
        swapped = pltpu.roll(second[:, cut], lanes // 2, 1)
        swapped = jnp.where(lane < lanes // 2, -swapped, swapped)
        spec = (first[:, cut] + swapped).astype(bf)
        out_ref[block, :, 0, :, :] = spec.reshape(groups, rows_per, lanes)


def spectra(slots, own_re, own_im, far_re, far_im, tables, shape, first, waves, slot, after, into):
    col_a, row_re, row_im = tables
    _, _, rows, cols = own_re.shape
    blocks, groups, _, rows_per, lanes = shape
    field = pl.BlockSpec((1, 1, rows, cols), lambda i, sl: (first + i, 0, 0, 0))
    partner = pl.BlockSpec((1, 1, rows, cols), lambda i, sl: (sl[first + i], 0, 0, 0))
    whole_col = pl.BlockSpec((2 * cols, 2 * cols), lambda i, sl: (0, 0))
    whole_row = pl.BlockSpec((rows, rows), lambda i, sl: (0, 0))
    flops = waves * (2 * rows * (2 * cols) * (2 * cols) + 2 * 2 * rows * rows * (2 * cols))
    extra = list(after) + ([] if into is None else [into])
    return pl.pallas_call(
        spectrum_kernel,
        out_shape=jax.ShapeDtypeStruct(shape, jnp.bfloat16),
        grid_spec=pltpu.PrefetchScalarGridSpec(
            num_scalar_prefetch=1,
            grid=(waves,),
            in_specs=[field, field, partner, partner, whole_col, whole_row, whole_row]
            + [pl.BlockSpec(memory_space=pl.ANY)] * len(extra),
            out_specs=pl.BlockSpec(
                (blocks, groups, 1, rows_per, lanes), lambda i, sl: (0, 0, slot + i, 0, 0)
            ),
        ),
        input_output_aliases={} if into is None else {8 + len(after): 0},
        compiler_params=pltpu.CompilerParams(vmem_limit_bytes=60 * 1024 * 1024),
        cost_estimate=pl.CostEstimate(
            flops=flops, transcendentals=0, bytes_accessed=waves * rows * cols * 12 + 12 * cols * cols
        ),
    )(slots, own_re, own_im, far_re, far_im, col_a, row_re, row_im, *extra)


def shards(hologram_real, hologram_imaginary, pair_slot, kernel_real, kernel_imaginary):
    fp = jnp.float32
    wave_devices = lax.axis_size("wave")
    angle_devices = lax.axis_size("angle")
    local_waves, local_angles, row_count, col_count = hologram_real.shape
    section_count = pair_slot.shape[0]
    depth_count = kernel_real.shape[3]
    row_real, row_imag = dft_tables(row_count)
    col_real, col_imag = dft_tables(col_count)
    tables = (column_tables(col_real, col_imag, wave_devices), row_real, row_imag)
    lanes = 2 * col_count // wave_devices
    rows_per = row_count // angle_devices

    def all_weights(kernel_part):
        block = kernel_part.reshape(
            wave_devices, local_waves, section_count, angle_devices, depth_count
        )
        return jnp.transpose(block, (0, 3, 2, 1, 4)).reshape(
            wave_devices * angle_devices, section_count * local_waves, depth_count
        )

    k_re = all_weights(kernel_real)
    k_im = all_weights(kernel_imaginary)
    received = [
        from_partner((hologram_real, hologram_imaginary), "wave", section_number)
        for section_number in range(section_count)
    ]
    total = section_count * local_waves
    small = local_waves // 2
    split = [(total - small, total), (0, total - small)]
    devices = wave_devices * angle_devices
    warm = lax.all_to_all(
        hologram_real[0, 0, :devices, :], ("wave", "angle"), 0, 0, tiled=True
    )
    warmed = [warm]
    volume = None
    for low, high in split:
        shape = (wave_devices, angle_devices, high - low, rows_per, lanes)
        send = None
        for section_number in range(section_count):
            lo = max(low, section_number * local_waves)
            hi = min(high, (section_number + 1) * local_waves)
            if lo >= hi:
                continue
            got_real, got_imag = received[section_number]
            after = [a for other, got in enumerate(received) if other != section_number for a in got]
            after = after + warmed
            warmed = []
            send = spectra(
                pair_slot[section_number],
                hologram_real,
                hologram_imaginary,
                got_real,
                got_imag,
                tables,
                shape,
                lo - section_number * local_waves,
                hi - lo,
                lo - low,
                after,
                send,
            )
        send = send.reshape(wave_devices * angle_devices, *send.shape[2:])
        got = lax.all_to_all(send, ("wave", "angle"), 0, 0, tiled=True)
        got = with_layout_constraint(got, Layout(tuple(range(got.ndim))))
        kr = k_re[:, low:high]
        ki = k_im[:, low:high]
        w_first = jnp.stack([kr, ki], axis=2).reshape(kr.shape[0], kr.shape[1], -1)
        w_second = jnp.stack([-ki, kr], axis=2).reshape(kr.shape[0], kr.shape[1], -1)
        both = jnp.concatenate([w_first, w_second], axis=2)
        t = jnp.einsum("swrn,swx->rnx", got, both, preferred_element_type=fp)
        half = got.shape[3] // 2
        width = w_first.shape[2]
        part = t[:, :half, :width] + t[:, half:, width:]
        volume = part if volume is None else volume + part
    return (volume[:, :, :depth_count], volume[:, :, depth_count:])


def solution(mesh):
    return jax.shard_map(
        shards,
        mesh=mesh,
        in_specs=(
            P("wave", "angle", None, None),
            P("wave", "angle", None, None),
            P(None, "wave"),
            P(),
            P(),
        ),
        out_specs=(P("angle", "wave", None), P("angle", "wave", None)),
        check_vma=False,
    )
```

```python
import functools
import math

import jax
import jax.numpy as jnp
from jax import lax
from jax.experimental import pallas as pl
from jax.experimental.layout import Layout, with_layout_constraint
from jax.experimental.pallas import tpu as pltpu
from jax.sharding import PartitionSpec as P


def from_partner(block, axis, bit):
    count = lax.axis_size(axis)
    route = []
    for low in range(count):
        high = low | 1 << bit
        if high != low and high < count:
            route += [(low, high), (high, low)]
    return lax.ppermute(block, axis, route)


def dft_tables(length):
    counter = jnp.arange(length, dtype=jnp.int32)
    product = counter[:, None] * counter[None, :] % length
    phase = product.astype(jnp.float32) * (2.0 * math.pi / length)
    factor = 1.0 / math.sqrt(length)
    return (
        (jnp.cos(phase) * factor).astype(jnp.bfloat16),
        (-jnp.sin(phase) * factor).astype(jnp.bfloat16),
    )


def column_tables(table_real, table_imag, blocks):
    rows = table_real.shape[0]
    er = table_real.reshape(rows, blocks, 1, -1)
    ei = table_imag.reshape(rows, blocks, 1, -1)

    def join(top, bottom):
        upper = jnp.concatenate(top, axis=2).reshape(rows, -1)
        lower = jnp.concatenate(bottom, axis=2).reshape(rows, -1)
        return jnp.concatenate([upper, lower], axis=0)

    return join([er, ei], [-ei, er])


def spectrum_kernel(
    slot_ref, own_re, own_im, far_re, far_im, col_a, row_re, row_im, *rest
):
    out_ref = rest[-1]
    fp = jnp.float32
    bf = jnp.bfloat16
    a_re = own_re[0, 0].astype(fp)
    a_im = own_im[0, 0].astype(fp)
    b_re = far_re[0, 0].astype(fp)
    b_im = far_im[0, 0].astype(fp)
    z_re = (a_re * b_re + a_im * b_im).astype(bf)
    z_im = (a_im * b_re - a_re * b_im).astype(bf)
    z = jnp.concatenate([z_re, z_im], axis=1)
    y = jnp.dot(z, col_a[...], preferred_element_type=fp).astype(bf)
    first = jnp.dot(row_re[...], y, preferred_element_type=fp)
    second = jnp.dot(row_im[...], y, preferred_element_type=fp)
    blocks, groups, _, rows_per, lanes = out_ref.shape
    lane = lax.broadcasted_iota(jnp.int32, (first.shape[0], lanes), 1)
    for block in range(blocks):
        cut = slice(block * lanes, (block + 1) * lanes)
        swapped = pltpu.roll(second[:, cut], lanes // 2, 1)
        swapped = jnp.where(lane < lanes // 2, -swapped, swapped)
        spec = (first[:, cut] + swapped).astype(bf)
        out_ref[block, :, 0, :, :] = spec.reshape(groups, rows_per, lanes)


def spectra(slots, own_re, own_im, far_re, far_im, tables, shape, first, waves, slot, after, into):
    col_a, row_re, row_im = tables
    _, _, rows, cols = own_re.shape
    blocks, groups, _, rows_per, lanes = shape
    field = pl.BlockSpec((1, 1, rows, cols), lambda i, sl: (first + i, 0, 0, 0))
    partner = pl.BlockSpec((1, 1, rows, cols), lambda i, sl: (sl[first + i], 0, 0, 0))
    whole_col = pl.BlockSpec((2 * cols, 2 * cols), lambda i, sl: (0, 0))
    whole_row = pl.BlockSpec((rows, rows), lambda i, sl: (0, 0))
    flops = waves * (2 * rows * (2 * cols) * (2 * cols) + 2 * 2 * rows * rows * (2 * cols))
    extra = list(after) + ([] if into is None else [into])
    return pl.pallas_call(
        spectrum_kernel,
        out_shape=jax.ShapeDtypeStruct(shape, jnp.bfloat16),
        grid_spec=pltpu.PrefetchScalarGridSpec(
            num_scalar_prefetch=1,
            grid=(waves,),
            in_specs=[field, field, partner, partner, whole_col, whole_row, whole_row]
            + [pl.BlockSpec(memory_space=pl.ANY)] * len(extra),
            out_specs=pl.BlockSpec(
                (blocks, groups, 1, rows_per, lanes), lambda i, sl: (0, 0, slot + i, 0, 0)
            ),
        ),
        input_output_aliases={} if into is None else {8 + len(after): 0},
        compiler_params=pltpu.CompilerParams(vmem_limit_bytes=60 * 1024 * 1024),
        cost_estimate=pl.CostEstimate(
            flops=flops, transcendentals=0, bytes_accessed=waves * rows * cols * 12 + 12 * cols * cols
        ),
    )(slots, own_re, own_im, far_re, far_im, col_a, row_re, row_im, *extra)


def shards(hologram_real, hologram_imaginary, pair_slot, kernel_real, kernel_imaginary):
    fp = jnp.float32
    wave_devices = lax.axis_size("wave")
    angle_devices = lax.axis_size("angle")
    local_waves, local_angles, row_count, col_count = hologram_real.shape
    section_count = pair_slot.shape[0]
    depth_count = kernel_real.shape[3]
    row_real, row_imag = dft_tables(row_count)
    col_real, col_imag = dft_tables(col_count)
    tables = (column_tables(col_real, col_imag, wave_devices), row_real, row_imag)
    lanes = 2 * col_count // wave_devices
    rows_per = row_count // angle_devices

    def all_weights(kernel_part):
        block = kernel_part.reshape(
            wave_devices, local_waves, section_count, angle_devices, depth_count
        )
        return jnp.transpose(block, (0, 3, 2, 1, 4)).reshape(
            wave_devices * angle_devices, section_count * local_waves, depth_count
        )

    k_re = all_weights(kernel_real)
    k_im = all_weights(kernel_imaginary)
    received = [
        from_partner((hologram_real, hologram_imaginary), "wave", section_number)
        for section_number in range(section_count)
    ]
    total = section_count * local_waves
    small = local_waves // 2
    split = [(total - small, total), (0, total - small)]
    devices = wave_devices * angle_devices
    warm = lax.all_to_all(
        hologram_real[0, 0, :devices, :], ("wave", "angle"), 0, 0, tiled=True
    )
    warmed = []
    volume = None
    for low, high in split:
        shape = (wave_devices, angle_devices, high - low, rows_per, lanes)
        send = None
        for section_number in range(section_count):
            lo = max(low, section_number * local_waves)
            hi = min(high, (section_number + 1) * local_waves)
            if lo >= hi:
                continue
            got_real, got_imag = received[section_number]
            after = [a for other, got in enumerate(received) if other != section_number for a in got]
            after = after + warmed
            warmed = []
            send = spectra(
                pair_slot[section_number],
                hologram_real,
                hologram_imaginary,
                got_real,
                got_imag,
                tables,
                shape,
                lo - section_number * local_waves,
                hi - lo,
                lo - low,
                after,
                send,
            )
        send = send.reshape(wave_devices * angle_devices, *send.shape[2:])
        got = lax.all_to_all(send, ("wave", "angle"), 0, 0, tiled=True)
        warmed = [warm] if low == split[0][0] else []
        got = with_layout_constraint(got, Layout(tuple(range(got.ndim))))
        kr = k_re[:, low:high]
        ki = k_im[:, low:high]
        w_first = jnp.stack([kr, ki], axis=2).reshape(kr.shape[0], kr.shape[1], -1)
        w_second = jnp.stack([-ki, kr], axis=2).reshape(kr.shape[0], kr.shape[1], -1)
        both = jnp.concatenate([w_first, w_second], axis=2)
        t = jnp.einsum("swrn,swx->rnx", got, both, preferred_element_type=fp)
        half = got.shape[3] // 2
        width = w_first.shape[2]
        part = t[:, :half, :width] + t[:, half:, width:]
        volume = part if volume is None else volume + part
    return (volume[:, :, :depth_count], volume[:, :, depth_count:])


def solution(mesh):
    return jax.shard_map(
        shards,
        mesh=mesh,
        in_specs=(
            P("wave", "angle", None, None),
            P("wave", "angle", None, None),
            P(None, "wave"),
            P(),
            P(),
        ),
        out_specs=(P("angle", "wave", None), P("angle", "wave", None)),
        check_vma=False,
    )
```

```python
import functools
import math

import jax
import jax.numpy as jnp
from jax import lax
from jax.experimental import pallas as pl
from jax.experimental.layout import Layout, with_layout_constraint
from jax.experimental.pallas import tpu as pltpu
from jax.sharding import PartitionSpec as P


def from_partner(block, axis, bit):
    count = lax.axis_size(axis)
    route = []
    for low in range(count):
        high = low | 1 << bit
        if high != low and high < count:
            route += [(low, high), (high, low)]
    return lax.ppermute(block, axis, route)


def dft_tables(length):
    counter = jnp.arange(length, dtype=jnp.int32)
    product = counter[:, None] * counter[None, :] % length
    phase = product.astype(jnp.float32) * (2.0 * math.pi / length)
    factor = 1.0 / math.sqrt(length)
    return (
        (jnp.cos(phase) * factor).astype(jnp.bfloat16),
        (-jnp.sin(phase) * factor).astype(jnp.bfloat16),
    )


def column_tables(table_real, table_imag, blocks):
    rows = table_real.shape[0]
    er = table_real.reshape(rows, blocks, 1, -1)
    ei = table_imag.reshape(rows, blocks, 1, -1)

    def join(top, bottom):
        upper = jnp.concatenate(top, axis=2).reshape(rows, -1)
        lower = jnp.concatenate(bottom, axis=2).reshape(rows, -1)
        return jnp.concatenate([upper, lower], axis=0)

    return join([er, ei], [-ei, er])


def spectrum_kernel(
    slot_ref, own_re, own_im, far_re, far_im, col_a, row_re, row_im, *rest
):
    out_ref = rest[-1]
    fp = jnp.float32
    bf = jnp.bfloat16
    a_re = own_re[0, 0].astype(fp)
    a_im = own_im[0, 0].astype(fp)
    b_re = far_re[0, 0].astype(fp)
    b_im = far_im[0, 0].astype(fp)
    z_re = (a_re * b_re + a_im * b_im).astype(bf)
    z_im = (a_im * b_re - a_re * b_im).astype(bf)
    z = jnp.concatenate([z_re, z_im], axis=1)
    y = jnp.dot(z, col_a[...], preferred_element_type=fp).astype(bf)
    first = jnp.dot(row_re[...], y, preferred_element_type=fp)
    second = jnp.dot(row_im[...], y, preferred_element_type=fp)
    blocks, groups, _, rows_per, lanes = out_ref.shape
    lane = lax.broadcasted_iota(jnp.int32, (first.shape[0], lanes), 1)
    for block in range(blocks):
        cut = slice(block * lanes, (block + 1) * lanes)
        swapped = pltpu.roll(second[:, cut], lanes // 2, 1)
        swapped = jnp.where(lane < lanes // 2, -swapped, swapped)
        spec = (first[:, cut] + swapped).astype(bf)
        out_ref[block, :, 0, :, :] = spec.reshape(groups, rows_per, lanes)


def spectra(slots, own_re, own_im, far_re, far_im, tables, shape, first, waves, slot, after, into):
    col_a, row_re, row_im = tables
    _, _, rows, cols = own_re.shape
    blocks, groups, _, rows_per, lanes = shape
    field = pl.BlockSpec((1, 1, rows, cols), lambda i, sl: (first + i, 0, 0, 0))
    partner = pl.BlockSpec((1, 1, rows, cols), lambda i, sl: (sl[first + i], 0, 0, 0))
    whole_col = pl.BlockSpec(memory_space=pltpu.VMEM)
    whole_row = pl.BlockSpec(memory_space=pltpu.VMEM)
    flops = waves * (2 * rows * (2 * cols) * (2 * cols) + 2 * 2 * rows * rows * (2 * cols))
    extra = list(after) + ([] if into is None else [into])
    return pl.pallas_call(
        spectrum_kernel,
        out_shape=jax.ShapeDtypeStruct(shape, jnp.bfloat16),
        grid_spec=pltpu.PrefetchScalarGridSpec(
            num_scalar_prefetch=1,
            grid=(waves,),
            in_specs=[field, field, partner, partner, whole_col, whole_row, whole_row]
            + [pl.BlockSpec(memory_space=pl.ANY)] * len(extra),
            out_specs=pl.BlockSpec(
                (blocks, groups, 1, rows_per, lanes), lambda i, sl: (0, 0, slot + i, 0, 0)
            ),
        ),
        input_output_aliases={} if into is None else {8 + len(after): 0},
        compiler_params=pltpu.CompilerParams(vmem_limit_bytes=60 * 1024 * 1024),
        cost_estimate=pl.CostEstimate(
            flops=flops, transcendentals=0, bytes_accessed=waves * rows * cols * 12 + 12 * cols * cols
        ),
    )(slots, own_re, own_im, far_re, far_im, col_a, row_re, row_im, *extra)


def shards(hologram_real, hologram_imaginary, pair_slot, kernel_real, kernel_imaginary):
    fp = jnp.float32
    wave_devices = lax.axis_size("wave")
    angle_devices = lax.axis_size("angle")
    local_waves, local_angles, row_count, col_count = hologram_real.shape
    section_count = pair_slot.shape[0]
    depth_count = kernel_real.shape[3]
    row_real, row_imag = dft_tables(row_count)
    col_real, col_imag = dft_tables(col_count)
    tables = (column_tables(col_real, col_imag, wave_devices), row_real, row_imag)
    lanes = 2 * col_count // wave_devices
    rows_per = row_count // angle_devices

    def all_weights(kernel_part):
        block = kernel_part.reshape(
            wave_devices, local_waves, section_count, angle_devices, depth_count
        )
        return jnp.transpose(block, (0, 3, 2, 1, 4)).reshape(
            wave_devices * angle_devices, section_count * local_waves, depth_count
        )

    k_re = all_weights(kernel_real)
    k_im = all_weights(kernel_imaginary)
    received = [
        from_partner((hologram_real, hologram_imaginary), "wave", section_number)
        for section_number in range(section_count)
    ]
    total = section_count * local_waves
    small = local_waves // 2
    split = [(total - small, total), (0, total - small)]
    volume = None
    for low, high in split:
        shape = (wave_devices, angle_devices, high - low, rows_per, lanes)
        send = None
        for section_number in range(section_count):
            lo = max(low, section_number * local_waves)
            hi = min(high, (section_number + 1) * local_waves)
            if lo >= hi:
                continue
            got_real, got_imag = received[section_number]
            after = [a for other, got in enumerate(received) if other != section_number for a in got]
            send = spectra(
                pair_slot[section_number],
                hologram_real,
                hologram_imaginary,
                got_real,
                got_imag,
                tables,
                shape,
                lo - section_number * local_waves,
                hi - lo,
                lo - low,
                after,
                send,
            )
        send = send.reshape(wave_devices * angle_devices, *send.shape[2:])
        got = lax.all_to_all(send, ("wave", "angle"), 0, 0, tiled=True)
        got = with_layout_constraint(got, Layout(tuple(range(got.ndim))))
        kr = k_re[:, low:high]
        ki = k_im[:, low:high]
        w_first = jnp.stack([kr, ki], axis=2).reshape(kr.shape[0], kr.shape[1], -1)
        w_second = jnp.stack([-ki, kr], axis=2).reshape(kr.shape[0], kr.shape[1], -1)
        both = jnp.concatenate([w_first, w_second], axis=2)
        t = jnp.einsum("swrn,swx->rnx", got, both, preferred_element_type=fp)
        half = got.shape[3] // 2
        width = w_first.shape[2]
        part = t[:, :half, :width] + t[:, half:, width:]
        volume = part if volume is None else volume + part
    return (volume[:, :, :depth_count], volume[:, :, depth_count:])


def solution(mesh):
    return jax.shard_map(
        shards,
        mesh=mesh,
        in_specs=(
            P("wave", "angle", None, None),
            P("wave", "angle", None, None),
            P(None, "wave"),
            P(),
            P(),
        ),
        out_specs=(P("angle", "wave", None), P("angle", "wave", None)),
        check_vma=False,
    )
```

```python
import functools
import math

import jax
import jax.numpy as jnp
from jax import lax
from jax.experimental import pallas as pl
from jax.experimental.layout import Layout, with_layout_constraint
from jax.experimental.pallas import tpu as pltpu
from jax.sharding import PartitionSpec as P


def from_partner(block, axis, bit):
    count = lax.axis_size(axis)
    route = []
    for low in range(count):
        high = low | 1 << bit
        if high != low and high < count:
            route += [(low, high), (high, low)]
    return lax.ppermute(block, axis, route)


def dft_tables(length):
    counter = jnp.arange(length, dtype=jnp.int32)
    product = counter[:, None] * counter[None, :] % length
    phase = product.astype(jnp.float32) * (2.0 * math.pi / length)
    factor = 1.0 / math.sqrt(length)
    return (
        (jnp.cos(phase) * factor).astype(jnp.bfloat16),
        (-jnp.sin(phase) * factor).astype(jnp.bfloat16),
    )


def column_tables(table_real, table_imag, blocks):
    rows = table_real.shape[0]
    er = table_real.reshape(rows, blocks, 1, -1)
    ei = table_imag.reshape(rows, blocks, 1, -1)

    def join(top, bottom):
        upper = jnp.concatenate(top, axis=2).reshape(rows, -1)
        lower = jnp.concatenate(bottom, axis=2).reshape(rows, -1)
        return jnp.concatenate([upper, lower], axis=0)

    return join([er, ei], [-ei, er])


def spectrum_kernel(
    slot_ref, own_re, own_im, far_re, far_im, col_a, row_re, row_im, *rest
):
    out_ref = rest[-1]
    fp = jnp.float32
    bf = jnp.bfloat16
    a_re = own_re[0, 0].astype(fp)
    a_im = own_im[0, 0].astype(fp)
    b_re = far_re[0, 0].astype(fp)
    b_im = far_im[0, 0].astype(fp)
    z_re = (a_re * b_re + a_im * b_im).astype(bf)
    z_im = (a_im * b_re - a_re * b_im).astype(bf)
    z = jnp.concatenate([z_re, z_im], axis=1)
    y = jnp.dot(z, col_a[...], preferred_element_type=fp).astype(bf)
    both = jnp.dot(
        jnp.concatenate([row_re[...], row_im[...]], axis=0), y, preferred_element_type=fp
    )
    n = row_re.shape[0]
    first = both[:n]
    second = both[n:]
    blocks, groups, _, rows_per, lanes = out_ref.shape
    lane = lax.broadcasted_iota(jnp.int32, (first.shape[0], lanes), 1)
    for block in range(blocks):
        cut = slice(block * lanes, (block + 1) * lanes)
        swapped = pltpu.roll(second[:, cut], lanes // 2, 1)
        swapped = jnp.where(lane < lanes // 2, -swapped, swapped)
        spec = (first[:, cut] + swapped).astype(bf)
        out_ref[block, :, 0, :, :] = spec.reshape(groups, rows_per, lanes)


def spectra(slots, own_re, own_im, far_re, far_im, tables, shape, first, waves, slot, after, into):
    col_a, row_re, row_im = tables
    _, _, rows, cols = own_re.shape
    blocks, groups, _, rows_per, lanes = shape
    field = pl.BlockSpec((1, 1, rows, cols), lambda i, sl: (first + i, 0, 0, 0))
    partner = pl.BlockSpec((1, 1, rows, cols), lambda i, sl: (sl[first + i], 0, 0, 0))
    whole_col = pl.BlockSpec((2 * cols, 2 * cols), lambda i, sl: (0, 0))
    whole_row = pl.BlockSpec((rows, rows), lambda i, sl: (0, 0))
    flops = waves * (2 * rows * (2 * cols) * (2 * cols) + 2 * 2 * rows * rows * (2 * cols))
    extra = list(after) + ([] if into is None else [into])
    return pl.pallas_call(
        spectrum_kernel,
        out_shape=jax.ShapeDtypeStruct(shape, jnp.bfloat16),
        grid_spec=pltpu.PrefetchScalarGridSpec(
            num_scalar_prefetch=1,
            grid=(waves,),
            in_specs=[field, field, partner, partner, whole_col, whole_row, whole_row]
            + [pl.BlockSpec(memory_space=pl.ANY)] * len(extra),
            out_specs=pl.BlockSpec(
                (blocks, groups, 1, rows_per, lanes), lambda i, sl: (0, 0, slot + i, 0, 0)
            ),
        ),
        input_output_aliases={} if into is None else {8 + len(after): 0},
        compiler_params=pltpu.CompilerParams(vmem_limit_bytes=60 * 1024 * 1024),
        cost_estimate=pl.CostEstimate(
            flops=flops, transcendentals=0, bytes_accessed=waves * rows * cols * 12 + 12 * cols * cols
        ),
    )(slots, own_re, own_im, far_re, far_im, col_a, row_re, row_im, *extra)


def shards(hologram_real, hologram_imaginary, pair_slot, kernel_real, kernel_imaginary):
    fp = jnp.float32
    wave_devices = lax.axis_size("wave")
    angle_devices = lax.axis_size("angle")
    local_waves, local_angles, row_count, col_count = hologram_real.shape
    section_count = pair_slot.shape[0]
    depth_count = kernel_real.shape[3]
    row_real, row_imag = dft_tables(row_count)
    col_real, col_imag = dft_tables(col_count)
    tables = (column_tables(col_real, col_imag, wave_devices), row_real, row_imag)
    lanes = 2 * col_count // wave_devices
    rows_per = row_count // angle_devices

    def all_weights(kernel_part):
        block = kernel_part.reshape(
            wave_devices, local_waves, section_count, angle_devices, depth_count
        )
        return jnp.transpose(block, (0, 3, 2, 1, 4)).reshape(
            wave_devices * angle_devices, section_count * local_waves, depth_count
        )

    k_re = all_weights(kernel_real)
    k_im = all_weights(kernel_imaginary)
    received = [
        from_partner((hologram_real, hologram_imaginary), "wave", section_number)
        for section_number in range(section_count)
    ]
    total = section_count * local_waves
    small = local_waves // 2
    split = [(total - small, total), (0, total - small)]
    volume = None
    for low, high in split:
        shape = (wave_devices, angle_devices, high - low, rows_per, lanes)
        send = None
        for section_number in range(section_count):
            lo = max(low, section_number * local_waves)
            hi = min(high, (section_number + 1) * local_waves)
            if lo >= hi:
                continue
            got_real, got_imag = received[section_number]
            after = [a for other, got in enumerate(received) if other != section_number for a in got]
            send = spectra(
                pair_slot[section_number],
                hologram_real,
                hologram_imaginary,
                got_real,
                got_imag,
                tables,
                shape,
                lo - section_number * local_waves,
                hi - lo,
                lo - low,
                after,
                send,
            )
        send = send.reshape(wave_devices * angle_devices, *send.shape[2:])
        got = lax.all_to_all(send, ("wave", "angle"), 0, 0, tiled=True)
        got = with_layout_constraint(got, Layout(tuple(range(got.ndim))))
        kr = k_re[:, low:high]
        ki = k_im[:, low:high]
        w_first = jnp.stack([kr, ki], axis=2).reshape(kr.shape[0], kr.shape[1], -1)
        w_second = jnp.stack([-ki, kr], axis=2).reshape(kr.shape[0], kr.shape[1], -1)
        both = jnp.concatenate([w_first, w_second], axis=2)
        t = jnp.einsum("swrn,swx->rnx", got, both, preferred_element_type=fp)
        half = got.shape[3] // 2
        width = w_first.shape[2]
        part = t[:, :half, :width] + t[:, half:, width:]
        volume = part if volume is None else volume + part
    return (volume[:, :, :depth_count], volume[:, :, depth_count:])


def solution(mesh):
    return jax.shard_map(
        shards,
        mesh=mesh,
        in_specs=(
            P("wave", "angle", None, None),
            P("wave", "angle", None, None),
            P(None, "wave"),
            P(),
            P(),
        ),
        out_specs=(P("angle", "wave", None), P("angle", "wave", None)),
        check_vma=False,
    )
```

```python
import functools
import math

import jax
import jax.numpy as jnp
from jax import lax
from jax.experimental import pallas as pl
from jax.experimental.layout import Layout, with_layout_constraint
from jax.experimental.pallas import tpu as pltpu
from jax.sharding import PartitionSpec as P


def from_partner(block, axis, bit):
    count = lax.axis_size(axis)
    route = []
    for low in range(count):
        high = low | 1 << bit
        if high != low and high < count:
            route += [(low, high), (high, low)]
    return lax.ppermute(block, axis, route)


def dft_tables(length):
    counter = jnp.arange(length, dtype=jnp.int32)
    product = counter[:, None] * counter[None, :] % length
    phase = product.astype(jnp.float32) * (2.0 * math.pi / length)
    factor = 1.0 / math.sqrt(length)
    return (
        (jnp.cos(phase) * factor).astype(jnp.bfloat16),
        (-jnp.sin(phase) * factor).astype(jnp.bfloat16),
    )


def column_tables(table_real, table_imag, blocks):
    rows = table_real.shape[0]
    er = table_real.reshape(rows, blocks, 1, -1)
    ei = table_imag.reshape(rows, blocks, 1, -1)

    def join(top, bottom):
        upper = jnp.concatenate(top, axis=2).reshape(rows, -1)
        lower = jnp.concatenate(bottom, axis=2).reshape(rows, -1)
        return jnp.concatenate([upper, lower], axis=0)

    return join([er, ei], [-ei, er])


def spectrum_kernel(
    slot_ref, own_re, own_im, far_re, far_im, col_a, row_re, row_im, *rest
):
    out_ref = rest[-1]
    fp = jnp.float32
    bf = jnp.bfloat16
    a_re = own_re[0, 0].astype(fp)
    a_im = own_im[0, 0].astype(fp)
    b_re = far_re[0, 0].astype(fp)
    b_im = far_im[0, 0].astype(fp)
    z_re = (a_re * b_re + a_im * b_im).astype(bf)
    z_im = (a_im * b_re - a_re * b_im).astype(bf)
    z = jnp.concatenate([z_re, z_im], axis=1)
    y = jnp.dot(z, col_a[...], preferred_element_type=fp).astype(bf)
    first = jnp.dot(row_re[...], y, preferred_element_type=fp)
    second = jnp.dot(row_im[...], y, preferred_element_type=fp)
    blocks, groups, _, rows_per, lanes = out_ref.shape
    lane = lax.broadcasted_iota(jnp.int32, (first.shape[0], lanes), 1)
    for block in range(blocks):
        cut = slice(block * lanes, (block + 1) * lanes)
        swapped = pltpu.roll(second[:, cut], lanes // 2, 1)
        swapped = jnp.where(lane < lanes // 2, -swapped, swapped)
        spec = (first[:, cut] + swapped).astype(bf)
        out_ref[block, :, 0, :, :] = spec.reshape(groups, rows_per, lanes)


def spectra(slots, own_re, own_im, far_re, far_im, tables, shape, first, waves, slot, after, into):
    col_a, row_re, row_im = tables
    _, _, rows, cols = own_re.shape
    blocks, groups, _, rows_per, lanes = shape
    field = pl.BlockSpec((1, 1, rows, cols), lambda i, sl: (first + i, 0, 0, 0))
    partner = pl.BlockSpec((1, 1, rows, cols), lambda i, sl: (sl[first + i], 0, 0, 0))
    whole_col = pl.BlockSpec((2 * cols, 2 * cols), lambda i, sl: (0, 0))
    whole_row = pl.BlockSpec((rows, rows), lambda i, sl: (0, 0))
    flops = waves * (2 * rows * (2 * cols) * (2 * cols) + 2 * 2 * rows * rows * (2 * cols))
    extra = list(after) + ([] if into is None else [into])
    return pl.pallas_call(
        spectrum_kernel,
        out_shape=jax.ShapeDtypeStruct(shape, jnp.bfloat16),
        grid_spec=pltpu.PrefetchScalarGridSpec(
            num_scalar_prefetch=1,
            grid=(waves,),
            in_specs=[field, field, partner, partner, whole_col, whole_row, whole_row]
            + [pl.BlockSpec(memory_space=pl.ANY)] * len(extra),
            out_specs=pl.BlockSpec(
                (blocks, groups, 1, rows_per, lanes), lambda i, sl: (0, 0, slot + i, 0, 0)
            ),
        ),
        input_output_aliases={} if into is None else {8 + len(after): 0},
        compiler_params=pltpu.CompilerParams(vmem_limit_bytes=60 * 1024 * 1024),
        cost_estimate=pl.CostEstimate(
            flops=flops, transcendentals=0, bytes_accessed=waves * rows * cols * 12 + 12 * cols * cols
        ),
    )(slots, own_re, own_im, far_re, far_im, col_a, row_re, row_im, *extra)


def shards(hologram_real, hologram_imaginary, pair_slot, kernel_real, kernel_imaginary):
    fp = jnp.float32
    wave_devices = lax.axis_size("wave")
    angle_devices = lax.axis_size("angle")
    local_waves, local_angles, row_count, col_count = hologram_real.shape
    section_count = pair_slot.shape[0]
    depth_count = kernel_real.shape[3]
    row_real, row_imag = dft_tables(row_count)
    col_real, col_imag = dft_tables(col_count)
    tables = (column_tables(col_real, col_imag, wave_devices), row_real, row_imag)
    lanes = 2 * col_count // wave_devices
    rows_per = row_count // angle_devices

    def all_weights(kernel_part):
        block = kernel_part.reshape(
            wave_devices, local_waves, section_count, angle_devices, depth_count
        )
        return jnp.transpose(block, (0, 3, 2, 1, 4)).reshape(
            wave_devices * angle_devices, section_count * local_waves, depth_count
        )

    k_re = all_weights(kernel_real)
    k_im = all_weights(kernel_imaginary)
    received = [
        from_partner((hologram_real, hologram_imaginary), "wave", section_number)
        for section_number in range(section_count)
    ]
    total = section_count * local_waves
    small = local_waves // 2
    split = [(total - small, total), (0, total - small)]
    volume = None
    for low, high in split:
        shape = (wave_devices, angle_devices, high - low, rows_per, lanes)
        send = None
        for section_number in range(section_count):
            lo = max(low, section_number * local_waves)
            hi = min(high, (section_number + 1) * local_waves)
            if lo >= hi:
                continue
            got_real, got_imag = received[section_number]
            after = [got[0] for other, got in enumerate(received) if other != section_number]
            send = spectra(
                pair_slot[section_number],
                hologram_real,
                hologram_imaginary,
                got_real,
                got_imag,
                tables,
                shape,
                lo - section_number * local_waves,
                hi - lo,
                lo - low,
                after,
                send,
            )
        send = send.reshape(wave_devices * angle_devices, *send.shape[2:])
        got = lax.all_to_all(send, ("wave", "angle"), 0, 0, tiled=True)
        got = with_layout_constraint(got, Layout(tuple(range(got.ndim))))
        kr = k_re[:, low:high]
        ki = k_im[:, low:high]
        w_first = jnp.stack([kr, ki], axis=2).reshape(kr.shape[0], kr.shape[1], -1)
        w_second = jnp.stack([-ki, kr], axis=2).reshape(kr.shape[0], kr.shape[1], -1)
        both = jnp.concatenate([w_first, w_second], axis=2)
        t = jnp.einsum("swrn,swx->rnx", got, both, preferred_element_type=fp)
        half = got.shape[3] // 2
        width = w_first.shape[2]
        part = t[:, :half, :width] + t[:, half:, width:]
        volume = part if volume is None else volume + part
    return (volume[:, :, :depth_count], volume[:, :, depth_count:])


def solution(mesh):
    return jax.shard_map(
        shards,
        mesh=mesh,
        in_specs=(
            P("wave", "angle", None, None),
            P("wave", "angle", None, None),
            P(None, "wave"),
            P(),
            P(),
        ),
        out_specs=(P("angle", "wave", None), P("angle", "wave", None)),
        check_vma=False,
    )
```

```python
import functools
import math

import jax
import jax.numpy as jnp
from jax import lax
from jax.experimental import pallas as pl
from jax.experimental.layout import Layout, with_layout_constraint
from jax.experimental.pallas import tpu as pltpu
from jax.sharding import PartitionSpec as P


def from_partner(block, axis, bit):
    count = lax.axis_size(axis)
    route = []
    for low in range(count):
        high = low | 1 << bit
        if high != low and high < count:
            route += [(low, high), (high, low)]
    return lax.ppermute(block, axis, route)


def dft_tables(length):
    counter = jnp.arange(length, dtype=jnp.int32)
    product = counter[:, None] * counter[None, :] % length
    phase = product.astype(jnp.float32) * (2.0 * math.pi / length)
    factor = 1.0 / math.sqrt(length)
    return (
        (jnp.cos(phase) * factor).astype(jnp.bfloat16),
        (-jnp.sin(phase) * factor).astype(jnp.bfloat16),
    )


def column_tables(table_real, table_imag, blocks):
    rows = table_real.shape[0]
    er = table_real.reshape(rows, blocks, 1, -1)
    ei = table_imag.reshape(rows, blocks, 1, -1)

    def join(top, bottom):
        upper = jnp.concatenate(top, axis=2).reshape(rows, -1)
        lower = jnp.concatenate(bottom, axis=2).reshape(rows, -1)
        return jnp.concatenate([upper, lower], axis=0)

    return join([er, ei], [-ei, er])


def spectrum_kernel(
    slot_ref, own_re, own_im, far_re, far_im, col_a, row_re, row_im, *rest
):
    out_ref = rest[-1]
    fp = jnp.float32
    bf = jnp.bfloat16
    a_re = own_re[0, 0].astype(fp)
    a_im = own_im[0, 0].astype(fp)
    b_re = far_re[0, 0].astype(fp)
    b_im = far_im[0, 0].astype(fp)
    z_re = (a_re * b_re + a_im * b_im).astype(bf)
    z_im = (a_im * b_re - a_re * b_im).astype(bf)
    z = jnp.concatenate([z_re, z_im], axis=1)
    y = jnp.dot(z, col_a[...], preferred_element_type=fp).astype(bf)
    first = jnp.dot(row_re[...], y, preferred_element_type=fp)
    second = jnp.dot(row_im[...], y, preferred_element_type=fp)
    blocks, groups, _, rows_per, lanes = out_ref.shape
    lane = lax.broadcasted_iota(jnp.int32, (first.shape[0], lanes), 1)
    for block in range(blocks):
        cut = slice(block * lanes, (block + 1) * lanes)
        swapped = pltpu.roll(second[:, cut], lanes // 2, 1)
        swapped = jnp.where(lane < lanes // 2, -swapped, swapped)
        spec = (first[:, cut] + swapped).astype(bf)
        out_ref[block, :, 0, :, :] = spec.reshape(groups, rows_per, lanes)


def spectra(slots, own_re, own_im, far_re, far_im, tables, shape, first, waves, slot, after, into):
    col_a, row_re, row_im = tables
    _, _, rows, cols = own_re.shape
    blocks, groups, _, rows_per, lanes = shape
    field = pl.BlockSpec((1, 1, rows, cols), lambda i, sl: (first + i, 0, 0, 0))
    partner = pl.BlockSpec((1, 1, rows, cols), lambda i, sl: (sl[first + i], 0, 0, 0))
    whole_col = pl.BlockSpec((2 * cols, 2 * cols), lambda i, sl: (0, 0))
    whole_row = pl.BlockSpec((rows, rows), lambda i, sl: (0, 0))
    flops = waves * (2 * rows * (2 * cols) * (2 * cols) + 2 * 2 * rows * rows * (2 * cols))
    extra = list(after) + ([] if into is None else [into])
    return pl.pallas_call(
        spectrum_kernel,
        out_shape=jax.ShapeDtypeStruct(shape, jnp.bfloat16),
        grid_spec=pltpu.PrefetchScalarGridSpec(
            num_scalar_prefetch=1,
            grid=(waves,),
            in_specs=[field, field, partner, partner, whole_col, whole_row, whole_row]
            + [pl.BlockSpec(memory_space=pl.ANY)] * len(extra),
            out_specs=pl.BlockSpec(
                (blocks, groups, 1, rows_per, lanes), lambda i, sl: (0, 0, slot + i, 0, 0)
            ),
        ),
        input_output_aliases={} if into is None else {8 + len(after): 0},
        compiler_params=pltpu.CompilerParams(vmem_limit_bytes=60 * 1024 * 1024),
        cost_estimate=pl.CostEstimate(
            flops=flops, transcendentals=0, bytes_accessed=waves * rows * cols * 12 + 12 * cols * cols
        ),
    )(slots, own_re, own_im, far_re, far_im, col_a, row_re, row_im, *extra)


def shards(hologram_real, hologram_imaginary, pair_slot, kernel_real, kernel_imaginary):
    fp = jnp.float32
    wave_devices = lax.axis_size("wave")
    angle_devices = lax.axis_size("angle")
    local_waves, local_angles, row_count, col_count = hologram_real.shape
    section_count = pair_slot.shape[0]
    depth_count = kernel_real.shape[3]
    row_real, row_imag = dft_tables(row_count)
    col_real, col_imag = dft_tables(col_count)
    tables = (column_tables(col_real, col_imag, wave_devices), row_real, row_imag)
    lanes = 2 * col_count // wave_devices
    rows_per = row_count // angle_devices

    def all_weights(kernel_part):
        block = kernel_part.reshape(
            wave_devices, local_waves, section_count, angle_devices, depth_count
        )
        return jnp.transpose(block, (0, 3, 2, 1, 4)).reshape(
            wave_devices * angle_devices, section_count * local_waves, depth_count
        )

    k_re = all_weights(kernel_real)
    k_im = all_weights(kernel_imaginary)
    received = [
        from_partner((hologram_real, hologram_imaginary), "wave", section_number)
        for section_number in range(section_count)
    ]
    total = section_count * local_waves
    small = local_waves // 2
    split = [(total - small, total), (0, total - small)]
    volume = None
    for low, high in split:
        shape = (wave_devices, angle_devices, high - low, rows_per, lanes)
        send = None
        for section_number in range(section_count):
            lo = max(low, section_number * local_waves)
            hi = min(high, (section_number + 1) * local_waves)
            if lo >= hi:
                continue
            got_real, got_imag = received[section_number]
            after = [got[0] for other, got in enumerate(received) if other != section_number]
            after = after if low == 0 else []
            send = spectra(
                pair_slot[section_number],
                hologram_real,
                hologram_imaginary,
                got_real,
                got_imag,
                tables,
                shape,
                lo - section_number * local_waves,
                hi - lo,
                lo - low,
                after,
                send,
            )
        send = send.reshape(wave_devices * angle_devices, *send.shape[2:])
        got = lax.all_to_all(send, ("wave", "angle"), 0, 0, tiled=True)
        got = with_layout_constraint(got, Layout(tuple(range(got.ndim))))
        kr = k_re[:, low:high]
        ki = k_im[:, low:high]
        w_first = jnp.stack([kr, ki], axis=2).reshape(kr.shape[0], kr.shape[1], -1)
        w_second = jnp.stack([-ki, kr], axis=2).reshape(kr.shape[0], kr.shape[1], -1)
        both = jnp.concatenate([w_first, w_second], axis=2)
        t = jnp.einsum("swrn,swx->rnx", got, both, preferred_element_type=fp)
        half = got.shape[3] // 2
        width = w_first.shape[2]
        part = t[:, :half, :width] + t[:, half:, width:]
        volume = part if volume is None else volume + part
    return (volume[:, :, :depth_count], volume[:, :, depth_count:])


def solution(mesh):
    return jax.shard_map(
        shards,
        mesh=mesh,
        in_specs=(
            P("wave", "angle", None, None),
            P("wave", "angle", None, None),
            P(None, "wave"),
            P(),
            P(),
        ),
        out_specs=(P("angle", "wave", None), P("angle", "wave", None)),
        check_vma=False,
    )
```
